256 devices in a mesh: sub: 128 (over x_lo, y, z, core), depth: 2 (over x_hi).
Axes of the slice: x: 4 (x_hi: 2, x_lo: 2; x = x_hi * 2 + x_lo), y: 4, z: 8, core: 2. Of those that a mesh axis runs over, the one named last changes fastest.
Arguments:
- recharge: float32 [128, 2, 40, 128], P('sub', 'depth'), may hold values from -6 to 6
- inv_diag: float32 [128, 2, 40, 128, 128], P('sub', 'depth')
- couple: bfloat16 [128, 2, 40, 6, 128, 128], P('sub', 'depth'), may hold values from -0.09716797 to 0.09716797
- col_index: int32 [128, 2, 40, 6], P('sub', 'depth'), may hold values from 0 to 41, as said below
- soil_id: int32 [128, 2, 40], P('sub', 'depth'), may hold values from 0 to 11
- field_id: int32 [128, 2, 40], P('sub', 'depth'), may hold values from 0 to 4999
- robin_table: float32 [12], replicated, may hold values from 0.05 to 0.2
- field_rate: float32 [5000], replicated, may hold values from 0.1 to 2
- matching: int32 [4, 128], replicated, may hold values from 0 to 127, as said below
- lambda_in: float32 [128, 2, 4, 2, 128], P('sub', 'depth'), may hold values from -6 to 6
Outputs:
- state: float32 [128, 2, 40, 128], P('sub', 'depth')
- robin_data: float32 [128, 2, 4, 2, 128], P('sub', 'depth')
The draws below stay inside these ranges and needn't reach their ends.
Inputs may be any that keep to these rules, and one draw needn't show every extreme that they name: Each row c pairs every subdomain s with another one, matching[c, s] != s, and matching[c, matching[c, s]] = s. `col_index`: A block row never names its own block; indices from 40 on name the other half's last 2 blocks in order.
All inputs are finite; a program needn't handle non-finite values.
Results may differ from the reference program's by a relative error of at most 0.0003.
Values sent between devices are 32-bit elements; how exact they have to be, the bound alone decides.
No kernel may reach another device: no remote copies, remote signals or barrier semaphores. Data moves between devices by JAX's collectives and lax.ppermute only.
A program may use at most 64 MiB of HBM per device.

```python
import math
import jax
import jax.numpy as jnp
from jax import lax

BLOCK = 64
UNK = 128
NB = 40
BW = 6
COLOURS = 4
IB = 2
G = 2
SWEEPS = 4
OUTER = 2
SOILS = 12
FIELDS = 5000
SUBS = 128
HALVES = 2


def draw_inv_diag(key, part):
    key_diag = jax.random.fold_in(key, 11)
    key_rest = jax.random.fold_in(key, 12)
    diag = jax.random.uniform(key_diag, (SUBS, HALVES, NB, UNK), jnp.float32, 0.5, 1.5)
    rest = jax.random.normal(key_rest, (SUBS, HALVES, NB, UNK, UNK), jnp.float32) * (0.3 / UNK ** 0.5)
    identity = jnp.eye(UNK, dtype=jnp.float32)
    return rest + diag[..., None] * identity


def draw_col_index(key, part):
    key_off = jax.random.fold_in(key, 21)
    offset = jax.random.randint(key_off, (SUBS, HALVES, NB, BW), 1, NB + G)
    rows = jnp.arange(NB, dtype=jnp.int32)[None, None, :, None]
    return ((rows + offset) % (NB + G)).astype(jnp.int32)


def draw_matching(key, part):
    rows = []
    for colour in range(COLOURS):
        order = jax.random.permutation(jax.random.fold_in(key, 31 + colour), SUBS).astype(jnp.int32)
        pairs = order.reshape(SUBS // 2, 2)
        partner = jnp.zeros((SUBS,), jnp.int32)
        partner = partner.at[pairs[:, 0]].set(pairs[:, 1])
        partner = partner.at[pairs[:, 1]].set(pairs[:, 0])
        rows.append(partner)
    return jnp.stack(rows, axis=0)


def place_ends(result, own_key, low, top_value):
    index_at = [jax.random.randint(jax.random.fold_in(own_key, axis), (), 0, length) for axis, length in enumerate(result.shape)]
    main_axis = result.shape.index(max(result.shape))
    next_to = index_at[:main_axis] + [(index_at[main_axis] + 1) % result.shape[main_axis]] + index_at[main_axis + 1:]
    return result.at[tuple(index_at)].set(low).at[tuple(next_to)].set(top_value)


def levels(key, shape, split, low, high):
    def one(axis_at, blocks):
        draws = jax.random.uniform(jax.random.fold_in(jax.random.fold_in(key, 6), axis_at), (blocks,), jnp.float32, low / len(split), high / len(split))
        return jnp.repeat(jnp.exp(draws), shape[axis_at] // blocks).reshape((-1,) + (1,) * (len(shape) - axis_at - 1))

    gain = one(*split[0])
    for cut in split[1:]:
        gain = gain * one(*cut)
    return gain


def gaussian(stream_key, dims, width, reach, shards=(), kind=jnp.bfloat16):
    loudness = levels(stream_key, dims, shards, -0.22, 0.18) if shards else 1.0
    drawn = jax.random.normal(stream_key, dims, jnp.float32) * width * loudness
    return jnp.minimum(jnp.maximum(drawn, -reach), reach).astype(kind)


def setup_inputs(seed: int = 0) -> dict:
    seeds = jax.random.split(jax.random.key(seed), 11)
    return {
        "recharge": gaussian(seeds[0], (SUBS, HALVES, NB, UNK), 1.0, 6.0, ((0, 128), (1, 2)), jnp.float32),
        "inv_diag": draw_inv_diag(jax.random.fold_in(seeds[10], 71), 0),
        "couple": gaussian(seeds[2], (SUBS, HALVES, NB, BW, UNK, UNK), (0.45 / (BW * UNK) ** 0.5), 0.09716797, ((0, 128), (1, 2))),
        "col_index": draw_col_index(jax.random.fold_in(seeds[10], 71), 0),
        "soil_id": place_ends(jax.random.randint(seeds[4], (SUBS, HALVES, NB), 0, SOILS), jax.random.fold_in(seeds[4], 1), 0, SOILS - 1).astype(jnp.int32),
        "field_id": place_ends(jax.random.randint(seeds[5], (SUBS, HALVES, NB), 0, FIELDS), jax.random.fold_in(seeds[5], 1), 0, FIELDS - 1).astype(jnp.int32),
        "robin_table": jnp.clip(jnp.exp(jax.random.uniform(seeds[6], (SOILS,), jnp.float32, math.log(0.05), math.log(0.2))), 0.05, 0.2),
        "field_rate": jnp.clip(jnp.exp(jax.random.uniform(seeds[7], (FIELDS,), jnp.float32, math.log(0.1), math.log(2.0))), 0.1, 2.0),
        "matching": draw_matching(jax.random.fold_in(seeds[10], 71), 0),
        "lambda_in": gaussian(seeds[9], (SUBS, HALVES, COLOURS, IB, UNK), 1.0, 6.0, ((0, 128), (1, 2)), jnp.float32),
    }


def reference(recharge, inv_diag, couple, col_index, soil_id, field_id, robin_table, field_rate, matching, lambda_in):
    iface = COLOURS * IB
    nitrate = (jnp.arange(UNK) >= BLOCK).astype(jnp.float32)
    rate = field_rate[field_id]
    rhs = recharge + rate[..., None] * nitrate
    p_face = robin_table[soil_id][:, :, :iface]
    robin_data = lambda_in
    state = jnp.zeros((SUBS, HALVES, NB, UNK), jnp.float32)
    tiles = couple.astype(jnp.float32)
    index = jnp.broadcast_to(col_index.reshape(SUBS, HALVES, NB * BW)[..., None], (SUBS, HALVES, NB * BW, UNK))
    for outer in range(OUTER):
        forcing = rhs + jnp.pad(robin_data.reshape(SUBS, HALVES, iface, UNK), ((0, 0), (0, 0), (0, NB - iface), (0, 0)))
        for sweep in range(SWEEPS):
            ghost = jnp.flip(state[:, :, NB - G:], axis=1)
            extended = jnp.concatenate([state, ghost], axis=2)
            neigh = jnp.take_along_axis(extended, index, axis=2).reshape(SUBS, HALVES, NB, BW, UNK)
            coupled = jnp.einsum('shrbij,shrbj->shri', tiles, neigh, precision=lax.Precision.HIGHEST)
            lagged = jnp.pad(p_face[..., None] * state[:, :, :iface], ((0, 0), (0, 0), (0, NB - iface), (0, 0)))
            state = jnp.einsum('shrij,shrj->shri', inv_diag, forcing - coupled - lagged, precision=lax.Precision.HIGHEST)
        outgoing = 2.0 * p_face.reshape(SUBS, HALVES, COLOURS, IB)[..., None] * state[:, :, :iface].reshape(SUBS, HALVES, COLOURS, IB, UNK) - robin_data
        robin_data = jnp.stack([outgoing[matching[colour], :, colour] for colour in range(COLOURS)], axis=2)
    return state, robin_data
```

```python
import jax
import jax.numpy as jnp
from jax import lax
from jax.sharding import PartitionSpec as P

G = 2
SWEEPS = 4
OUTER = 2


def partner(block, axis, bit):
    count = lax.axis_size(axis)
    route = []
    for low in range(count):
        high = low | 1 << bit
        if high != low and high < count:
            route += [(low, high), (high, low)]
    return lax.ppermute(block, axis, route)


def doubling_order(bits):
    if bits == 7:
        return [3, 5, 2, 6, 4, 1, 0]
    return list(range(bits - 1, -1, -1))


def exchange(outgoing, partners):
    count = lax.axis_size("sub")
    bits = count.bit_length() - 1
    me = lax.axis_index("sub")
    if 1 << bits != count:
        every = lax.all_gather(outgoing, "sub", axis=0, tiled=False)
        return every[partners, jnp.arange(outgoing.shape[0])]
    order = doubling_order(bits)
    held = outgoing[None]
    for bit in order:
        route = [(low, low ^ (1 << bit)) for low in range(count)]
        held = jnp.concatenate([held, lax.ppermute(held, "sub", route)], axis=0)
    flipped = partners ^ me
    entry = jnp.zeros_like(partners)
    for step, bit in enumerate(order):
        entry = entry | (((flipped >> bit) & 1) << step)
    return held[entry, jnp.arange(outgoing.shape[0])]


def per_device(
    recharge,
    inv_diag,
    couple,
    col_index,
    soil_id,
    field_id,
    robin_table,
    field_rate,
    matching,
    lambda_in,
):
    blocks = recharge.shape[2]
    width = recharge.shape[3]
    colours = lambda_in.shape[2]
    per_colour = lambda_in.shape[3]
    iface = colours * per_colour
    nitrate = (jnp.arange(width) >= width // 2).astype(jnp.float32)
    rate = jnp.take(field_rate, field_id[0, 0], axis=0)
    rhs = recharge[0, 0] + rate[:, None] * nitrate
    soil_hits = soil_id[0, 0][:, None] == jnp.arange(robin_table.shape[0], dtype=jnp.int32)[None, :]
    p_block = jnp.sum(jnp.where(soil_hits, robin_table[None, :], 0.0), axis=1)
    p_face = p_block[:iface]
    inverse = inv_diag[0, 0]
    tiles = couple[0, 0].astype(jnp.float32)
    columns = col_index[0, 0]
    partners = lax.dynamic_index_in_dim(matching, lax.axis_index("sub"), axis=1, keepdims=False)
    robin_data = lambda_in[0, 0]
    state = jnp.zeros((blocks, width), jnp.float32)
    filler = jnp.zeros((blocks - iface, width), jnp.float32)
    for outer in range(OUTER):
        forcing = rhs + jnp.concatenate([robin_data.reshape(iface, width), filler], axis=0)
        for sweep in range(SWEEPS):
            ghost = partner(state[blocks - G :], "depth", 0)
            extended = jnp.concatenate([state, ghost], axis=0)
            neigh = jnp.take(extended, columns, axis=0)
            coupled = jnp.einsum("rbij,rbj->ri", tiles, neigh, precision=lax.Precision.HIGHEST)
            lagged = jnp.concatenate([p_face[:, None] * state[:iface], filler], axis=0)
            state = jnp.einsum(
                "rij,rj->ri", inverse, forcing - coupled - lagged, precision=lax.Precision.HIGHEST
            )
        outgoing = (
            2.0
            * p_face.reshape(colours, per_colour)[..., None]
            * state[:iface].reshape(colours, per_colour, width)
            - robin_data
        )
        robin_data = exchange(outgoing, partners)
    return (state[None, None], robin_data[None, None])


def solution(mesh):
    placed = (
        P("sub", "depth", None, None),
        P("sub", "depth", None, None, None),
        P("sub", "depth", None, None, None, None),
        P("sub", "depth", None, None),
        P("sub", "depth", None),
        P("sub", "depth", None),
        P(),
        P(),
        P(),
        P("sub", "depth", None, None, None),
    )
    return jax.shard_map(
        per_device,
        mesh=mesh,
        in_specs=placed,
        out_specs=(P("sub", "depth", None, None), P("sub", "depth", None, None, None)),
        check_vma=False,
    )
```

```python
import jax
import jax.numpy as jnp
from jax import lax
from jax.sharding import PartitionSpec as P

G = 2
SWEEPS = 4
OUTER = 2


def partner(block, axis, bit):
    count = lax.axis_size(axis)
    route = []
    for low in range(count):
        high = low | 1 << bit
        if high != low and high < count:
            route += [(low, high), (high, low)]
    return lax.ppermute(block, axis, route)


def doubling_order(bits):
    if bits == 7:
        return [3, 5, 2, 6, 4, 1, 0]
    return list(range(bits - 1, -1, -1))


def exchange(outgoing, partners):
    count = lax.axis_size("sub")
    bits = count.bit_length() - 1
    me = lax.axis_index("sub")
    if 1 << bits != count:
        every = lax.all_gather(outgoing, "sub", axis=0, tiled=False)
        return every[partners, jnp.arange(outgoing.shape[0])]
    order = doubling_order(bits)
    held = outgoing[None]
    for bit in order:
        route = [(low, low ^ (1 << bit)) for low in range(count)]
        held = jnp.concatenate([held, lax.ppermute(held, "sub", route)], axis=0)
    flipped = partners ^ me
    entry = jnp.zeros_like(partners)
    for step, bit in enumerate(order):
        entry = entry | (((flipped >> bit) & 1) << step)
    return held[entry, jnp.arange(outgoing.shape[0])]


def per_device(
    recharge,
    inv_diag,
    couple,
    col_index,
    soil_id,
    field_id,
    robin_table,
    field_rate,
    matching,
    lambda_in,
):
    blocks = recharge.shape[2]
    width = recharge.shape[3]
    colours = lambda_in.shape[2]
    per_colour = lambda_in.shape[3]
    iface = colours * per_colour
    nitrate = (jnp.arange(width) >= width // 2).astype(jnp.float32)
    rate = jnp.take(field_rate, field_id[0, 0], axis=0)
    rhs = recharge[0, 0] + rate[:, None] * nitrate
    soil_hits = soil_id[0, 0][:, None] == jnp.arange(robin_table.shape[0], dtype=jnp.int32)[None, :]
    p_block = jnp.sum(jnp.where(soil_hits, robin_table[None, :], 0.0), axis=1)
    p_face = p_block[:iface]
    inverse = inv_diag[0, 0]
    tiles = couple[0, 0].astype(jnp.float32)
    columns = col_index[0, 0]
    partners = lax.dynamic_index_in_dim(matching, lax.axis_index("sub"), axis=1, keepdims=False)
    robin_data = lambda_in[0, 0]
    head = slice(blocks - G, blocks)
    body = slice(0, blocks - G)
    lag_rows = min(iface, blocks - G)

    def rows_update(rows, state, ghost, forcing):
        extended = jnp.concatenate([state, ghost], axis=0)
        neigh = jnp.take(extended, columns[rows], axis=0)
        coupled = jnp.einsum("rbij,rbj->ri", tiles[rows], neigh, precision=lax.Precision.HIGHEST)
        rhs_rows = forcing[rows] - coupled
        if rows.start < lag_rows:
            lagged = p_face[rows.start:lag_rows, None] * state[rows.start:lag_rows]
            lagged = jnp.concatenate([lagged, jnp.zeros((rows.stop - lag_rows, width), jnp.float32)], axis=0)
            rhs_rows = rhs_rows - lagged
        return jnp.einsum("rij,rj->ri", inverse[rows], rhs_rows, precision=lax.Precision.HIGHEST)

    def first_update(rows, forcing):
        return jnp.einsum("rij,rj->ri", inverse[rows], forcing[rows], precision=lax.Precision.HIGHEST)

    state = None
    ghost = None
    for outer in range(OUTER):
        forcing = jnp.concatenate([rhs[:iface] + robin_data.reshape(iface, width), rhs[iface:]], axis=0)
        for sweep in range(SWEEPS):
            if state is None:
                top = first_update(head, forcing)
                sent = partner(top, "depth", 0)
                rest = first_update(body, forcing)
            else:
                top = rows_update(head, state, ghost, forcing)
                sent = partner(top, "depth", 0)
                rest = rows_update(body, state, ghost, forcing)
            ghost = sent
            state = jnp.concatenate([rest, top], axis=0)
        outgoing = (
            2.0
            * p_face.reshape(colours, per_colour)[..., None]
            * state[:iface].reshape(colours, per_colour, width)
            - robin_data
        )
        robin_data = exchange(outgoing, partners)
    return (state[None, None], robin_data[None, None])


def solution(mesh):
    placed = (
        P("sub", "depth", None, None),
        P("sub", "depth", None, None, None),
        P("sub", "depth", None, None, None, None),
        P("sub", "depth", None, None),
        P("sub", "depth", None),
        P("sub", "depth", None),
        P(),
        P(),
        P(),
        P("sub", "depth", None, None, None),
    )
    return jax.shard_map(
        per_device,
        mesh=mesh,
        in_specs=placed,
        out_specs=(P("sub", "depth", None, None), P("sub", "depth", None, None, None)),
        check_vma=False,
    )
```

```python
import jax
import jax.numpy as jnp
from jax import lax
from jax.sharding import PartitionSpec as P

G = 2
SWEEPS = 4
OUTER = 2


def partner(block, axis, bit):
    count = lax.axis_size(axis)
    route = []
    for low in range(count):
        high = low | 1 << bit
        if high != low and high < count:
            route += [(low, high), (high, low)]
    return lax.ppermute(block, axis, route)


def exchange_rounds(bits):
    if bits == 7:
        return [(1, 3), (4, 2), (6, 1), (0, 1)]
    return [(bit, 1) for bit in range(bits - 1, -1, -1)]


def exchange(outgoing, partners):
    count = lax.axis_size("sub")
    bits = count.bit_length() - 1
    me = lax.axis_index("sub")
    if 1 << bits != count:
        every = lax.all_gather(outgoing, "sub", axis=0, tiled=False)
        return every[partners, jnp.arange(outgoing.shape[0])]
    rounds = exchange_rounds(bits)
    held = outgoing[None]
    for shift, width in rounds:
        pieces = [held]
        for step in range(1, 1 << width):
            route = [(low, low ^ (step << shift)) for low in range(count)]
            pieces.append(lax.ppermute(held, "sub", route))
        held = jnp.concatenate(pieces, axis=0)
    flipped = partners ^ me
    entry = jnp.zeros_like(partners)
    stride = 1
    for shift, width in rounds:
        entry = entry + ((flipped >> shift) & ((1 << width) - 1)) * stride
        stride = stride << width
    return held[entry, jnp.arange(outgoing.shape[0])]


def per_device(
    recharge,
    inv_diag,
    couple,
    col_index,
    soil_id,
    field_id,
    robin_table,
    field_rate,
    matching,
    lambda_in,
):
    blocks = recharge.shape[2]
    width = recharge.shape[3]
    colours = lambda_in.shape[2]
    per_colour = lambda_in.shape[3]
    iface = colours * per_colour
    nitrate = (jnp.arange(width) >= width // 2).astype(jnp.float32)
    rate = jnp.take(field_rate, field_id[0, 0], axis=0)
    rhs = recharge[0, 0] + rate[:, None] * nitrate
    soil_hits = soil_id[0, 0][:, None] == jnp.arange(robin_table.shape[0], dtype=jnp.int32)[None, :]
    p_block = jnp.sum(jnp.where(soil_hits, robin_table[None, :], 0.0), axis=1)
    p_face = p_block[:iface]
    inverse = inv_diag[0, 0]
    tiles = couple[0, 0].astype(jnp.float32)
    columns = col_index[0, 0]
    partners = lax.dynamic_index_in_dim(matching, lax.axis_index("sub"), axis=1, keepdims=False)
    robin_data = lambda_in[0, 0]
    head = slice(blocks - G, blocks)
    body = slice(0, blocks - G)
    lag_rows = min(iface, blocks - G)

    def rows_update(rows, state, ghost, forcing):
        extended = jnp.concatenate([state, ghost], axis=0)
        neigh = jnp.take(extended, columns[rows], axis=0)
        coupled = jnp.einsum("rbij,rbj->ri", tiles[rows], neigh, precision=lax.Precision.HIGHEST)
        rhs_rows = forcing[rows] - coupled
        if rows.start < lag_rows:
            lagged = p_face[rows.start:lag_rows, None] * state[rows.start:lag_rows]
            lagged = jnp.concatenate([lagged, jnp.zeros((rows.stop - lag_rows, width), jnp.float32)], axis=0)
            rhs_rows = rhs_rows - lagged
        return jnp.einsum("rij,rj->ri", inverse[rows], rhs_rows, precision=lax.Precision.HIGHEST)

    def first_update(rows, forcing):
        return jnp.einsum("rij,rj->ri", inverse[rows], forcing[rows], precision=lax.Precision.HIGHEST)

    state = None
    ghost = None
    for outer in range(OUTER):
        forcing = jnp.concatenate([rhs[:iface] + robin_data.reshape(iface, width), rhs[iface:]], axis=0)
        for sweep in range(SWEEPS):
            if state is None:
                top = first_update(head, forcing)
                sent = partner(top, "depth", 0)
                rest = first_update(body, forcing)
            else:
                top = rows_update(head, state, ghost, forcing)
                sent = partner(top, "depth", 0)
                rest = rows_update(body, state, ghost, forcing)
            ghost = sent
            state = jnp.concatenate([rest, top], axis=0)
        outgoing = (
            2.0
            * p_face.reshape(colours, per_colour)[..., None]
            * state[:iface].reshape(colours, per_colour, width)
            - robin_data
        )
        robin_data = exchange(outgoing, partners)
    return (state[None, None], robin_data[None, None])


def solution(mesh):
    placed = (
        P("sub", "depth", None, None),
        P("sub", "depth", None, None, None),
        P("sub", "depth", None, None, None, None),
        P("sub", "depth", None, None),
        P("sub", "depth", None),
        P("sub", "depth", None),
        P(),
        P(),
        P(),
        P("sub", "depth", None, None, None),
    )
    return jax.shard_map(
        per_device,
        mesh=mesh,
        in_specs=placed,
        out_specs=(P("sub", "depth", None, None), P("sub", "depth", None, None, None)),
        check_vma=False,
    )
```

```python
import jax
import jax.numpy as jnp
from jax import lax
from jax.sharding import PartitionSpec as P

G = 2
SWEEPS = 4
OUTER = 2


def partner(block, axis, bit):
    count = lax.axis_size(axis)
    route = []
    for low in range(count):
        high = low | 1 << bit
        if high != low and high < count:
            route += [(low, high), (high, low)]
    return lax.ppermute(block, axis, route)


def doubling_order(bits):
    if bits == 7:
        return [3, 5, 2, 6, 4, 1, 0]
    return list(range(bits - 1, -1, -1))


def exchange(outgoing, partners):
    count = lax.axis_size("sub")
    bits = count.bit_length() - 1
    me = lax.axis_index("sub")
    if 1 << bits != count:
        every = lax.all_gather(outgoing, "sub", axis=0, tiled=False)
        return every[partners, jnp.arange(outgoing.shape[0])]
    order = doubling_order(bits)
    held = outgoing[None]
    for bit in order:
        route = [(low, low ^ (1 << bit)) for low in range(count)]
        held = jnp.concatenate([held, lax.ppermute(held, "sub", route)], axis=0)
    flipped = partners ^ me
    entry = jnp.zeros_like(partners)
    for step, bit in enumerate(order):
        entry = entry | (((flipped >> bit) & 1) << step)
    return held[entry, jnp.arange(outgoing.shape[0])]


def per_device(
    recharge,
    inv_diag,
    couple,
    col_index,
    soil_id,
    field_id,
    robin_table,
    field_rate,
    matching,
    lambda_in,
):
    blocks = recharge.shape[2]
    width = recharge.shape[3]
    colours = lambda_in.shape[2]
    per_colour = lambda_in.shape[3]
    iface = colours * per_colour
    nitrate = (jnp.arange(width) >= width // 2).astype(jnp.float32)
    rate = jnp.take(field_rate, field_id[0, 0], axis=0)
    rhs = recharge[0, 0] + rate[:, None] * nitrate
    soil_hits = soil_id[0, 0][:, None] == jnp.arange(robin_table.shape[0], dtype=jnp.int32)[None, :]
    p_block = jnp.sum(jnp.where(soil_hits, robin_table[None, :], 0.0), axis=1)
    p_face = p_block[:iface]
    inverse = inv_diag[0, 0]
    tiles = couple[0, 0].astype(jnp.float32)
    columns = col_index[0, 0]
    partners = lax.dynamic_index_in_dim(matching, lax.axis_index("sub"), axis=1, keepdims=False)
    robin_data = lambda_in[0, 0]
    head = slice(blocks - G, blocks)
    body = slice(0, blocks - G)
    lag_rows = min(iface, blocks - G)

    def forcing_rows(rows, robin_data):
        if rows.stop <= iface:
            return rhs[rows] + robin_data.reshape(iface, width)[rows]
        if rows.start >= iface:
            return rhs[rows]
        return jnp.concatenate([forcing_rows(slice(rows.start, iface), robin_data), rhs[iface:rows.stop]], axis=0)

    def rows_update(rows, state, ghost, robin_data):
        forcing = forcing_rows(rows, robin_data)
        if state is None:
            return jnp.einsum("rij,rj->ri", inverse[rows], forcing, precision=lax.Precision.HIGHEST)
        extended = jnp.concatenate([state, ghost], axis=0)
        neigh = jnp.take(extended, columns[rows], axis=0)
        coupled = jnp.einsum("rbij,rbj->ri", tiles[rows], neigh, precision=lax.Precision.HIGHEST)
        rhs_rows = forcing - coupled
        if rows.start < lag_rows:
            lagged = p_face[rows.start:lag_rows, None] * state[rows.start:lag_rows]
            if rows.stop > lag_rows:
                lagged = jnp.concatenate([lagged, jnp.zeros((rows.stop - lag_rows, width), jnp.float32)], axis=0)
            rhs_rows = rhs_rows - lagged
        return jnp.einsum("rij,rj->ri", inverse[rows], rhs_rows, precision=lax.Precision.HIGHEST)

    face = slice(0, lag_rows)
    middle = slice(lag_rows, blocks - G)
    state = None
    ghost = None
    for outer in range(OUTER):
        for sweep in range(SWEEPS):
            split = sweep == SWEEPS - 1 or (sweep == 0 and outer > 0)
            top = rows_update(head, state, ghost, robin_data)
            sent = partner(top, "depth", 0) if outer < OUTER - 1 or sweep < SWEEPS - 1 else None
            if split:
                low = rows_update(face, state, ghost, robin_data)
                mid = rows_update(middle, state, ghost, robin_data)
                state = jnp.concatenate([low, mid, top], axis=0)
            else:
                state = jnp.concatenate([rows_update(body, state, ghost, robin_data), top], axis=0)
            ghost = sent
        outgoing = (
            2.0
            * p_face.reshape(colours, per_colour)[..., None]
            * state[:iface].reshape(colours, per_colour, width)
            - robin_data
        )
        robin_data = exchange(outgoing, partners)
    return (state[None, None], robin_data[None, None])


def solution(mesh):
    placed = (
        P("sub", "depth", None, None),
        P("sub", "depth", None, None, None),
        P("sub", "depth", None, None, None, None),
        P("sub", "depth", None, None),
        P("sub", "depth", None),
        P("sub", "depth", None),
        P(),
        P(),
        P(),
        P("sub", "depth", None, None, None),
    )
    return jax.shard_map(
        per_device,
        mesh=mesh,
        in_specs=placed,
        out_specs=(P("sub", "depth", None, None), P("sub", "depth", None, None, None)),
        check_vma=False,
    )
```

```python
import functools

import jax
import jax.numpy as jnp
from jax import lax
from jax.experimental import pallas as pl
from jax.sharding import PartitionSpec as P

G = 2
SWEEPS = 4
OUTER = 2


def partner(block, axis, bit):
    count = lax.axis_size(axis)
    route = []
    for low in range(count):
        high = low | 1 << bit
        if high != low and high < count:
            route += [(low, high), (high, low)]
    return lax.ppermute(block, axis, route)


def sweep_kernel(*refs, coupled_terms):
    if coupled_terms:
        c_ref, inv_ref, x_ref, f_ref, o_ref = refs
    else:
        inv_ref, f_ref, o_ref = refs
    rows = inv_ref.shape[0]
    for r in range(rows):
        y = f_ref[r]
        if coupled_terms:
            xr = x_ref[r]
            acc = None
            for b in range(c_ref.shape[1]):
                term = c_ref[r, b].astype(jnp.float32) * xr[b:b + 1, :]
                acc = term if acc is None else acc + term
            y = y - jnp.sum(acc.T, axis=0, keepdims=True)
        o_ref[r] = jnp.sum((inv_ref[r] * y).T, axis=0, keepdims=True)


def block_sweep(inv, f, tile=None, neigh=None, rows=8, first=0):
    blocks, width = f.shape[0], f.shape[2]
    count = (blocks - first * rows) // rows
    at = lambda g: g + first
    operands, specs = [], []
    if tile is not None:
        bands = tile.shape[1]
        operands += [tile]
        specs += [pl.BlockSpec((rows, bands, width, width), lambda g: (at(g), 0, 0, 0))]
    operands += [inv]
    specs += [pl.BlockSpec((rows, width, width), lambda g: (at(g), 0, 0))]
    if neigh is not None:
        operands += [neigh]
        specs += [pl.BlockSpec((rows, bands, width), lambda g: (at(g), 0, 0))]
    operands += [f]
    specs += [pl.BlockSpec((rows, 1, width), lambda g: (at(g), 0, 0))]
    done = count * rows
    bands_now = tile.shape[1] if tile is not None else 0
    cost = pl.CostEstimate(
        flops=2 * done * width * width * (bands_now + 1),
        transcendentals=0,
        bytes_accessed=done * width * width * (2 * bands_now + 4),
    )
    out = pl.pallas_call(
        functools.partial(sweep_kernel, coupled_terms=tile is not None),
        grid=(count,),
        in_specs=specs,
        out_specs=pl.BlockSpec((rows, 1, width), lambda g: (at(g), 0, 0)),
        out_shape=jax.ShapeDtypeStruct((blocks, 1, width), jnp.float32),
        cost_estimate=cost,
    )(*operands)
    return out[first * rows:first * rows + done, 0]


def doubling_order(bits):
    if bits == 7:
        return [3, 5, 2, 6, 4, 1, 0]
    return list(range(bits - 1, -1, -1))


def exchange(outgoing, partners):
    count = lax.axis_size("sub")
    bits = count.bit_length() - 1
    me = lax.axis_index("sub")
    if 1 << bits != count:
        every = lax.all_gather(outgoing, "sub", axis=0, tiled=False)
        return every[partners, jnp.arange(outgoing.shape[0])]
    order = doubling_order(bits)
    held = outgoing[None]
    for bit in order:
        route = [(low, low ^ (1 << bit)) for low in range(count)]
        held = jnp.concatenate([held, lax.ppermute(held, "sub", route)], axis=0)
    flipped = partners ^ me
    entry = jnp.zeros_like(partners)
    for step, bit in enumerate(order):
        entry = entry | (((flipped >> bit) & 1) << step)
    return held[entry, jnp.arange(outgoing.shape[0])]


def per_device(
    recharge,
    inv_diag,
    couple,
    col_index,
    soil_id,
    field_id,
    robin_table,
    field_rate,
    matching,
    lambda_in,
):
    blocks = recharge.shape[2]
    width = recharge.shape[3]
    colours = lambda_in.shape[2]
    per_colour = lambda_in.shape[3]
    iface = colours * per_colour
    nitrate = (jnp.arange(width) >= width // 2).astype(jnp.float32)
    rate = jnp.take(field_rate, field_id[0, 0], axis=0)
    rhs = recharge[0, 0] + rate[:, None] * nitrate
    soil_hits = soil_id[0, 0][:, None] == jnp.arange(robin_table.shape[0], dtype=jnp.int32)[None, :]
    p_block = jnp.sum(jnp.where(soil_hits, robin_table[None, :], 0.0), axis=1)
    p_face = p_block[:iface]
    inverse = inv_diag[0, 0]
    columns = col_index[0, 0]
    partners = lax.dynamic_index_in_dim(matching, lax.axis_index("sub"), axis=1, keepdims=False)
    robin_data = lambda_in[0, 0]

    def sweep_rows(state, ghost, forcing, rows, first):
        if state is None:
            return block_sweep(inverse, forcing[:, None], rows=rows, first=first)
        lagged = jnp.concatenate([p_face[:, None] * state[:iface], jnp.zeros((blocks - iface, width), jnp.float32)], axis=0)
        extended = jnp.concatenate([state, ghost], axis=0)
        neigh = jnp.take(extended, columns, axis=0)
        return block_sweep(inverse, (forcing - lagged)[:, None], couple[0, 0], neigh, rows=rows, first=first)

    state = None
    ghost = None
    for outer in range(OUTER):
        forcing = jnp.concatenate([rhs[:iface] + robin_data.reshape(iface, width), rhs[iface:]], axis=0)
        for sweep in range(SWEEPS):
            top = sweep_rows(state, ghost, forcing, G, (blocks - G) // G)
            sent = partner(top, "depth", 0)
            rest = sweep_rows(state, ghost, forcing, 8, 0)[: blocks - G]
            ghost = sent
            state = jnp.concatenate([rest, top], axis=0)
        outgoing = (
            2.0
            * p_face.reshape(colours, per_colour)[..., None]
            * state[:iface].reshape(colours, per_colour, width)
            - robin_data
        )
        robin_data = exchange(outgoing, partners)
    return (state[None, None], robin_data[None, None])


def solution(mesh):
    placed = (
        P("sub", "depth", None, None),
        P("sub", "depth", None, None, None),
        P("sub", "depth", None, None, None, None),
        P("sub", "depth", None, None),
        P("sub", "depth", None),
        P("sub", "depth", None),
        P(),
        P(),
        P(),
        P("sub", "depth", None, None, None),
    )
    return jax.shard_map(
        per_device,
        mesh=mesh,
        in_specs=placed,
        out_specs=(P("sub", "depth", None, None), P("sub", "depth", None, None, None)),
        check_vma=False,
    )
```

```python
import functools

import jax
import jax.numpy as jnp
from jax import lax
from jax.experimental import pallas as pl
from jax.experimental.pallas import tpu as pltpu
from jax.sharding import PartitionSpec as P

G = 2
SWEEPS = 4
OUTER = 2


def partner(block, axis, bit):
    count = lax.axis_size(axis)
    route = []
    for low in range(count):
        high = low | 1 << bit
        if high != low and high < count:
            route += [(low, high), (high, low)]
    return lax.ppermute(block, axis, route)


def sweep_kernel(*refs, coupled_terms, first, blocks):
    if coupled_terms:
        cols_ref, c_ref, inv_ref, state_ref, ghost_ref, f_ref, p_ref, o_ref = refs
    else:
        inv_ref, f_ref, o_ref = refs
    rows = inv_ref.shape[0]
    base = (pl.program_id(0) + first) * rows
    for r in range(rows):
        y = f_ref[r]
        if coupled_terms:
            bands = c_ref.shape[1]
            row = base + r
            acc = None
            for b in range(bands):
                col = cols_ref[row * bands + b]
                own = state_ref[jnp.minimum(col, blocks - 1)]
                other = ghost_ref[jnp.maximum(col - blocks, 0)]
                xb = jnp.where(col >= blocks, other, own)
                term = c_ref[r, b].astype(jnp.float32) * xb
                acc = term if acc is None else acc + term
            y = y - jnp.sum(acc.T, axis=0, keepdims=True)
            y = y - p_ref[r] * state_ref[row]
        o_ref[r] = jnp.sum((inv_ref[r] * y).T, axis=0, keepdims=True)


def block_sweep(inv, forcing, rows, first, count, coupling=None):
    blocks, width = forcing.shape[0], forcing.shape[2]
    at = lambda g, *_: (g + first, 0, 0)
    if coupling is None:
        operands = [inv, forcing]
        specs = [pl.BlockSpec((rows, width, width), at), pl.BlockSpec((rows, 1, width), at)]
        prefetch = 0
        bands = 0
    else:
        cols, tile, state, ghost, prows = coupling
        bands = tile.shape[1]
        operands = [cols, tile, inv, state, ghost, forcing, prows]
        specs = [
            pl.BlockSpec((rows, bands, width, width), lambda g, *_: (g + first, 0, 0, 0)),
            pl.BlockSpec((rows, width, width), at),
            pl.BlockSpec(state.shape, lambda g, *_: (0, 0, 0)),
            pl.BlockSpec(ghost.shape, lambda g, *_: (0, 0, 0)),
            pl.BlockSpec((rows, 1, width), at),
            pl.BlockSpec((rows, 1, width), at),
        ]
        prefetch = 1
    done = count * rows
    grid_spec = pltpu.PrefetchScalarGridSpec(
        num_scalar_prefetch=prefetch,
        grid=(count,),
        in_specs=specs,
        out_specs=pl.BlockSpec((rows, 1, width), lambda g, *_: (g, 0, 0)),
    )
    return pl.pallas_call(
        functools.partial(sweep_kernel, coupled_terms=coupling is not None, first=first, blocks=blocks),
        grid_spec=grid_spec,
        out_shape=jax.ShapeDtypeStruct((done, 1, width), jnp.float32),
        cost_estimate=pl.CostEstimate(
            flops=2 * done * width * width * (bands + 1),
            transcendentals=0,
            bytes_accessed=done * width * width * (2 * bands + 4),
        ),
    )(*operands)


def doubling_order(bits):
    if bits == 7:
        return [3, 5, 2, 6, 4, 1, 0]
    return list(range(bits - 1, -1, -1))


def exchange(outgoing, partners):
    count = lax.axis_size("sub")
    bits = count.bit_length() - 1
    me = lax.axis_index("sub")
    if 1 << bits != count:
        every = lax.all_gather(outgoing, "sub", axis=0, tiled=False)
        return every[partners, jnp.arange(outgoing.shape[0])]
    order = doubling_order(bits)
    held = outgoing[None]
    for bit in order:
        route = [(low, low ^ (1 << bit)) for low in range(count)]
        held = jnp.concatenate([held, lax.ppermute(held, "sub", route)], axis=0)
    flipped = partners ^ me
    entry = jnp.zeros_like(partners)
    for step, bit in enumerate(order):
        entry = entry | (((flipped >> bit) & 1) << step)
    return held[entry, jnp.arange(outgoing.shape[0])]


def per_device(
    recharge,
    inv_diag,
    couple,
    col_index,
    soil_id,
    field_id,
    robin_table,
    field_rate,
    matching,
    lambda_in,
):
    blocks = recharge.shape[2]
    width = recharge.shape[3]
    colours = lambda_in.shape[2]
    per_colour = lambda_in.shape[3]
    iface = colours * per_colour
    nitrate = (jnp.arange(width) >= width // 2).astype(jnp.float32)
    rate = jnp.take(field_rate, field_id[0, 0], axis=0)
    rhs = recharge[0, 0] + rate[:, None] * nitrate
    soil_hits = soil_id[0, 0][:, None] == jnp.arange(robin_table.shape[0], dtype=jnp.int32)[None, :]
    p_block = jnp.sum(jnp.where(soil_hits, robin_table[None, :], 0.0), axis=1)
    p_face = p_block[:iface]
    inverse = inv_diag[0, 0]
    columns = col_index[0, 0]
    partners = lax.dynamic_index_in_dim(matching, lax.axis_index("sub"), axis=1, keepdims=False)
    robin_data = lambda_in[0, 0]

    flat_columns = columns.reshape(-1)
    prows = jnp.concatenate([p_face, jnp.zeros((blocks - iface,), jnp.float32)])[:, None, None] * jnp.ones((1, 1, width), jnp.float32)

    def sweep_rows(state, ghost, forcing, rows, first, count):
        if state is None:
            return block_sweep(inverse, forcing, rows, first, count)
        coupling = (flat_columns, couple[0, 0], state, ghost, prows)
        return block_sweep(inverse, forcing, rows, first, count, coupling)

    head_forcing = rhs[:, None]
    state = None
    ghost = None
    for outer in range(OUTER):
        forcing = jnp.concatenate([rhs[:iface] + robin_data.reshape(iface, width), rhs[iface:]], axis=0)[:, None]
        for sweep in range(SWEEPS):
            top = sweep_rows(state, ghost, head_forcing if blocks - G >= iface else forcing, G, (blocks - G) // G, 1)
            sent = partner(top, "depth", 0)
            state = sweep_rows(state, ghost, forcing, 8, 0, blocks // 8)
            ghost = sent
        state2 = state[:, 0]
        outgoing = (
            2.0
            * p_face.reshape(colours, per_colour)[..., None]
            * state2[:iface].reshape(colours, per_colour, width)
            - robin_data
        )
        robin_data = exchange(outgoing, partners)
    return (state[:, 0][None, None], robin_data[None, None])


def solution(mesh):
    placed = (
        P("sub", "depth", None, None),
        P("sub", "depth", None, None, None),
        P("sub", "depth", None, None, None, None),
        P("sub", "depth", None, None),
        P("sub", "depth", None),
        P("sub", "depth", None),
        P(),
        P(),
        P(),
        P("sub", "depth", None, None, None),
    )
    return jax.shard_map(
        per_device,
        mesh=mesh,
        in_specs=placed,
        out_specs=(P("sub", "depth", None, None), P("sub", "depth", None, None, None)),
        check_vma=False,
    )
```

```python
import functools

import jax
import jax.numpy as jnp
from jax import lax
from jax.experimental import pallas as pl
from jax.experimental.pallas import tpu as pltpu
from jax.sharding import PartitionSpec as P

G = 2
SWEEPS = 4
OUTER = 2


def partner(block, axis, bit):
    count = lax.axis_size(axis)
    route = []
    for low in range(count):
        high = low | 1 << bit
        if high != low and high < count:
            route += [(low, high), (high, low)]
    return lax.ppermute(block, axis, route)


def sweep_kernel(*refs, coupled_terms, first, blocks):
    if coupled_terms:
        cols_ref, c_ref, inv_ref, state_ref, ghost_ref, f_ref, p_ref, o_ref = refs
    else:
        inv_ref, f_ref, o_ref = refs
    rows = inv_ref.shape[0]
    base = (pl.program_id(0) + first) * rows
    for r in range(rows):
        y = f_ref[r]
        if coupled_terms:
            bands = c_ref.shape[1]
            row = base + r
            acc = None
            for b in range(bands):
                col = cols_ref[row * bands + b]
                own = state_ref[jnp.minimum(col, blocks - 1)]
                other = ghost_ref[jnp.maximum(col - blocks, 0)]
                xb = jnp.where(col >= blocks, other, own)
                term = c_ref[r, b].astype(jnp.float32) * xb
                acc = term if acc is None else acc + term
            y = y - jnp.sum(acc.T, axis=0, keepdims=True)
            y = y - p_ref[r] * state_ref[row]
        o_ref[r] = jnp.sum((inv_ref[r] * y).T, axis=0, keepdims=True)


def block_sweep(inv, forcing, rows, first, count, coupling=None):
    blocks, width = forcing.shape[0], forcing.shape[2]
    at = lambda g, *_: (g + first, 0, 0)
    if coupling is None:
        operands = [inv, forcing]
        specs = [pl.BlockSpec((rows, width, width), at), pl.BlockSpec((rows, 1, width), at)]
        prefetch = 0
        bands = 0
    else:
        cols, tile, state, ghost, prows = coupling
        bands = tile.shape[1]
        operands = [cols, tile, inv, state, ghost, forcing, prows]
        specs = [
            pl.BlockSpec((rows, bands, width, width), lambda g, *_: (g + first, 0, 0, 0)),
            pl.BlockSpec((rows, width, width), at),
            pl.BlockSpec(state.shape, lambda g, *_: (0, 0, 0)),
            pl.BlockSpec(ghost.shape, lambda g, *_: (0, 0, 0)),
            pl.BlockSpec((rows, 1, width), at),
            pl.BlockSpec((rows, 1, width), at),
        ]
        prefetch = 1
    done = count * rows
    grid_spec = pltpu.PrefetchScalarGridSpec(
        num_scalar_prefetch=prefetch,
        grid=(count,),
        in_specs=specs,
        out_specs=pl.BlockSpec((rows, 1, width), lambda g, *_: (g, 0, 0)),
    )
    return pl.pallas_call(
        functools.partial(sweep_kernel, coupled_terms=coupling is not None, first=first, blocks=blocks),
        grid_spec=grid_spec,
        out_shape=jax.ShapeDtypeStruct((done, 1, width), jnp.float32),
        cost_estimate=pl.CostEstimate(
            flops=2 * done * width * width * (bands + 1),
            transcendentals=0,
            bytes_accessed=done * width * width * (2 * bands + 4),
        ),
    )(*operands)


def doubling_order(bits):
    if bits == 7:
        return [3, 5, 2, 6, 4, 1, 0]
    return list(range(bits - 1, -1, -1))


def exchange(outgoing, partners, tie=None, midway=None):
    count = lax.axis_size("sub")
    bits = count.bit_length() - 1
    me = lax.axis_index("sub")
    extra = None
    if tie is not None:
        outgoing, tie = lax.optimization_barrier((outgoing, tie))
    if 1 << bits != count:
        every = lax.all_gather(outgoing, "sub", axis=0, tiled=False)
        if midway is not None:
            extra = midway()
        return every[partners, jnp.arange(outgoing.shape[0])], extra
    order = doubling_order(bits)
    held = outgoing[None]
    for step, bit in enumerate(order):
        route = [(low, low ^ (1 << bit)) for low in range(count)]
        held = jnp.concatenate([held, lax.ppermute(held, "sub", route)], axis=0)
        if midway is not None and step == min(2, len(order) - 1):
            extra = midway()
            held, extra = lax.optimization_barrier((held, extra))
    flipped = partners ^ me
    entry = jnp.zeros_like(partners)
    for step, bit in enumerate(order):
        entry = entry | (((flipped >> bit) & 1) << step)
    return held[entry, jnp.arange(outgoing.shape[0])], extra


def per_device(
    recharge,
    inv_diag,
    couple,
    col_index,
    soil_id,
    field_id,
    robin_table,
    field_rate,
    matching,
    lambda_in,
):
    blocks = recharge.shape[2]
    width = recharge.shape[3]
    colours = lambda_in.shape[2]
    per_colour = lambda_in.shape[3]
    iface = colours * per_colour
    nitrate = (jnp.arange(width) >= width // 2).astype(jnp.float32)
    rate = jnp.take(field_rate, field_id[0, 0], axis=0)
    rhs = recharge[0, 0] + rate[:, None] * nitrate
    soil_hits = soil_id[0, 0][:, None] == jnp.arange(robin_table.shape[0], dtype=jnp.int32)[None, :]
    p_block = jnp.sum(jnp.where(soil_hits, robin_table[None, :], 0.0), axis=1)
    p_face = p_block[:iface]
    inverse = inv_diag[0, 0]
    columns = col_index[0, 0]
    partners = lax.dynamic_index_in_dim(matching, lax.axis_index("sub"), axis=1, keepdims=False)
    robin_data = lambda_in[0, 0]

    flat_columns = columns.reshape(-1)
    prows = jnp.concatenate([p_face, jnp.zeros((blocks - iface,), jnp.float32)])[:, None, None] * jnp.ones((1, 1, width), jnp.float32)

    def sweep_rows(state, ghost, forcing, rows, first, count):
        if state is None:
            return block_sweep(inverse, forcing, rows, first, count)
        coupling = (flat_columns, couple[0, 0], state, ghost, prows)
        return block_sweep(inverse, forcing, rows, first, count, coupling)

    head_forcing = rhs[:, None]
    head_source = lambda forcing: head_forcing if blocks - G >= iface else forcing
    pending = None
    state = None
    ghost = None
    for outer in range(OUTER):
        forcing = jnp.concatenate([rhs[:iface] + robin_data.reshape(iface, width), rhs[iface:]], axis=0)[:, None]
        for sweep in range(SWEEPS):
            if pending is not None:
                top, pending = pending, None
            else:
                top = sweep_rows(state, ghost, head_source(forcing), G, (blocks - G) // G, 1)
            sent = partner(top, "depth", 0)
            state = sweep_rows(state, ghost, forcing, 8, 0, blocks // 8)
            ghost = sent
        state2 = state[:, 0]
        outgoing = (
            2.0
            * p_face.reshape(colours, per_colour)[..., None]
            * state2[:iface].reshape(colours, per_colour, width)
            - robin_data
        )
        if outer < OUTER - 1 and blocks - G >= iface:
            ahead = lambda state=state, ghost=ghost: sweep_rows(state, ghost, head_forcing, G, (blocks - G) // G, 1)
            robin_data, pending = exchange(outgoing, partners, tie=top, midway=ahead)
        else:
            robin_data, _ = exchange(outgoing, partners)
    return (state[:, 0][None, None], robin_data[None, None])


def solution(mesh):
    placed = (
        P("sub", "depth", None, None),
        P("sub", "depth", None, None, None),
        P("sub", "depth", None, None, None, None),
        P("sub", "depth", None, None),
        P("sub", "depth", None),
        P("sub", "depth", None),
        P(),
        P(),
        P(),
        P("sub", "depth", None, None, None),
    )
    return jax.shard_map(
        per_device,
        mesh=mesh,
        in_specs=placed,
        out_specs=(P("sub", "depth", None, None), P("sub", "depth", None, None, None)),
        check_vma=False,
    )
```

```python
import functools

import jax
import jax.numpy as jnp
from jax import lax
from jax.experimental import pallas as pl
from jax.experimental.pallas import tpu as pltpu
from jax.sharding import PartitionSpec as P

G = 2
SWEEPS = 4
OUTER = 2


def partner(block, axis, bit):
    count = lax.axis_size(axis)
    route = []
    for low in range(count):
        high = low | 1 << bit
        if high != low and high < count:
            route += [(low, high), (high, low)]
    return lax.ppermute(block, axis, route)


def sweep_kernel(*refs, coupled_terms, first, blocks):
    if coupled_terms:
        cols_ref, c_ref, inv_ref, state_ref, ghost_ref, f_ref, p_ref, o_ref = refs
    else:
        inv_ref, f_ref, o_ref = refs
    rows = inv_ref.shape[0]
    base = (pl.program_id(0) + first) * rows
    for r in range(rows):
        y = f_ref[r]
        if coupled_terms:
            bands = c_ref.shape[1]
            row = base + r
            acc = None
            for b in range(bands):
                col = cols_ref[row * bands + b]
                own = state_ref[jnp.minimum(col, blocks - 1)]
                other = ghost_ref[jnp.maximum(col - blocks, 0)]
                xb = jnp.where(col >= blocks, other, own)
                term = c_ref[r, b].astype(jnp.float32) * xb
                acc = term if acc is None else acc + term
            y = y - jnp.sum(acc.T, axis=0, keepdims=True)
            y = y - p_ref[r] * state_ref[row]
        o_ref[r] = jnp.sum((inv_ref[r] * y).T, axis=0, keepdims=True)


def block_sweep(inv, forcing, rows, first, count, coupling=None):
    blocks, width = forcing.shape[0], forcing.shape[2]
    at = lambda g, *_: (g + first, 0, 0)
    if coupling is None:
        operands = [inv, forcing]
        specs = [pl.BlockSpec((rows, width, width), at), pl.BlockSpec((rows, 1, width), at)]
        prefetch = 0
        bands = 0
    else:
        cols, tile, state, ghost, prows = coupling
        bands = tile.shape[1]
        operands = [cols, tile, inv, state, ghost, forcing, prows]
        specs = [
            pl.BlockSpec((rows, bands, width, width), lambda g, *_: (g + first, 0, 0, 0)),
            pl.BlockSpec((rows, width, width), at),
            pl.BlockSpec(state.shape, lambda g, *_: (0, 0, 0)),
            pl.BlockSpec(ghost.shape, lambda g, *_: (0, 0, 0)),
            pl.BlockSpec((rows, 1, width), at),
            pl.BlockSpec((rows, 1, width), at),
        ]
        prefetch = 1
    done = count * rows
    grid_spec = pltpu.PrefetchScalarGridSpec(
        num_scalar_prefetch=prefetch,
        grid=(count,),
        in_specs=specs,
        out_specs=pl.BlockSpec((rows, 1, width), lambda g, *_: (g, 0, 0)),
    )
    return pl.pallas_call(
        functools.partial(sweep_kernel, coupled_terms=coupling is not None, first=first, blocks=blocks),
        grid_spec=grid_spec,
        out_shape=jax.ShapeDtypeStruct((done, 1, width), jnp.float32),
        cost_estimate=pl.CostEstimate(
            flops=2 * done * width * width * (bands + 1),
            transcendentals=0,
            bytes_accessed=done * width * width * (2 * bands + 4),
        ),
    )(*operands)


def doubling_order(bits):
    if bits == 7:
        return [3, 5, 2, 6, 4, 1, 0]
    return list(range(bits - 1, -1, -1))


def exchange(outgoing, partners, tie=None, hooks=()):
    count = lax.axis_size("sub")
    bits = count.bit_length() - 1
    me = lax.axis_index("sub")
    extra = [None] * len(hooks)
    if tie is not None:
        outgoing, tie = lax.optimization_barrier((outgoing, tie))
    if 1 << bits != count:
        every = lax.all_gather(outgoing, "sub", axis=0, tiled=False)
        extra = [hook() for _, hook in hooks]
        return every[partners, jnp.arange(outgoing.shape[0])], extra
    order = doubling_order(bits)
    held = outgoing[None]
    for step, bit in enumerate(order):
        route = [(low, low ^ (1 << bit)) for low in range(count)]
        held = jnp.concatenate([held, lax.ppermute(held, "sub", route)], axis=0)
        for index, (at, hook) in enumerate(hooks):
            if step == min(at, len(order) - 1):
                extra[index] = hook()
                held, extra[index] = lax.optimization_barrier((held, extra[index]))
    flipped = partners ^ me
    entry = jnp.zeros_like(partners)
    for step, bit in enumerate(order):
        entry = entry | (((flipped >> bit) & 1) << step)
    return held[entry, jnp.arange(outgoing.shape[0])], extra


def per_device(
    recharge,
    inv_diag,
    couple,
    col_index,
    soil_id,
    field_id,
    robin_table,
    field_rate,
    matching,
    lambda_in,
):
    blocks = recharge.shape[2]
    width = recharge.shape[3]
    colours = lambda_in.shape[2]
    per_colour = lambda_in.shape[3]
    iface = colours * per_colour
    nitrate = (jnp.arange(width) >= width // 2).astype(jnp.float32)
    rate = jnp.take(field_rate, field_id[0, 0], axis=0)
    rhs = recharge[0, 0] + rate[:, None] * nitrate
    soil_hits = soil_id[0, 0][:, None] == jnp.arange(robin_table.shape[0], dtype=jnp.int32)[None, :]
    p_block = jnp.sum(jnp.where(soil_hits, robin_table[None, :], 0.0), axis=1)
    p_face = p_block[:iface]
    inverse = inv_diag[0, 0]
    columns = col_index[0, 0]
    partners = lax.dynamic_index_in_dim(matching, lax.axis_index("sub"), axis=1, keepdims=False)
    robin_data = lambda_in[0, 0]

    flat_columns = columns.reshape(-1)
    prows = jnp.concatenate([p_face, jnp.zeros((blocks - iface,), jnp.float32)])[:, None, None] * jnp.ones((1, 1, width), jnp.float32)

    def sweep_rows(state, ghost, forcing, rows, first, count):
        if state is None:
            return block_sweep(inverse, forcing, rows, first, count)
        coupling = (flat_columns, couple[0, 0], state, ghost, prows)
        return block_sweep(inverse, forcing, rows, first, count, coupling)

    head_forcing = rhs[:, None]
    head_source = lambda forcing: head_forcing if blocks - G >= iface else forcing
    pending = None
    upper = None
    state = None
    ghost = None
    face_blocks = -(-iface // 8)
    split_ok = face_blocks * 8 <= blocks - G and blocks % 8 == 0 and blocks - G >= iface

    def upper_rows(state, ghost, forcing):
        return sweep_rows(state, ghost, forcing, 8, face_blocks, blocks // 8 - face_blocks)

    for outer in range(OUTER):
        forcing = jnp.concatenate([rhs[:iface] + robin_data.reshape(iface, width), rhs[iface:]], axis=0)[:, None]
        for sweep in range(SWEEPS):
            if pending is not None:
                top, pending = pending, None
            else:
                top = sweep_rows(state, ghost, head_source(forcing), G, (blocks - G) // G, 1)
            sent = partner(top, "depth", 0)
            final = outer == OUTER - 1 and sweep == SWEEPS - 1
            if upper is not None:
                low = sweep_rows(state, ghost, forcing, 8, 0, face_blocks)
                state = jnp.concatenate([low, upper], axis=0)
                upper = None
            elif final and split_ok and state is not None:
                low = sweep_rows(state, ghost, forcing, 8, 0, face_blocks)
                later = (state, ghost, forcing)
                state = low
            else:
                state = sweep_rows(state, ghost, forcing, 8, 0, blocks // 8)
            ghost = sent
        state2 = state[:, 0]
        outgoing = (
            2.0
            * p_face.reshape(colours, per_colour)[..., None]
            * state2[:iface].reshape(colours, per_colour, width)
            - robin_data
        )
        if outer < OUTER - 1 and split_ok:
            ahead = lambda state=state, ghost=ghost: sweep_rows(state, ghost, head_forcing, G, (blocks - G) // G, 1)
            rest = lambda state=state, ghost=ghost: upper_rows(state, ghost, head_forcing)
            robin_data, (pending, upper) = exchange(outgoing, partners, tie=top, hooks=((2, ahead), (4, rest)))
        elif outer == OUTER - 1 and split_ok:
            rest = lambda: upper_rows(*later)
            robin_data, (upper,) = exchange(outgoing, partners, hooks=((1, rest),))
            state = jnp.concatenate([state, upper], axis=0)
        else:
            robin_data, _ = exchange(outgoing, partners)
    return (state[:, 0][None, None], robin_data[None, None])


def solution(mesh):
    placed = (
        P("sub", "depth", None, None),
        P("sub", "depth", None, None, None),
        P("sub", "depth", None, None, None, None),
        P("sub", "depth", None, None),
        P("sub", "depth", None),
        P("sub", "depth", None),
        P(),
        P(),
        P(),
        P("sub", "depth", None, None, None),
    )
    return jax.shard_map(
        per_device,
        mesh=mesh,
        in_specs=placed,
        out_specs=(P("sub", "depth", None, None), P("sub", "depth", None, None, None)),
        check_vma=False,
    )
```

```python
import functools

import jax
import jax.numpy as jnp
from jax import lax
from jax.experimental import pallas as pl
from jax.experimental.pallas import tpu as pltpu
from jax.sharding import PartitionSpec as P

G = 2
SWEEPS = 4
OUTER = 2


def partner(block, axis, bit):
    count = lax.axis_size(axis)
    route = []
    for low in range(count):
        high = low | 1 << bit
        if high != low and high < count:
            route += [(low, high), (high, low)]
    return lax.ppermute(block, axis, route)


def sweep_kernel(*refs, coupled_terms, first, blocks):
    if coupled_terms:
        cols_ref, c_ref, inv_ref, state_ref, ghost_ref, f_ref, p_ref, o_ref = refs
    else:
        inv_ref, f_ref, o_ref = refs
    rows = inv_ref.shape[0]
    base = (pl.program_id(0) + first) * rows
    for r in range(rows):
        y = f_ref[r]
        if coupled_terms:
            bands = c_ref.shape[1]
            row = base + r
            acc = None
            for b in range(bands):
                col = cols_ref[row * bands + b]
                own = state_ref[jnp.minimum(col, blocks - 1)]
                other = ghost_ref[jnp.maximum(col - blocks, 0)]
                xb = jnp.where(col >= blocks, other, own)
                term = c_ref[r, b].astype(jnp.float32) * xb
                acc = term if acc is None else acc + term
            y = y - jnp.sum(acc.T, axis=0, keepdims=True)
            y = y - p_ref[r] * state_ref[row]
        o_ref[r] = jnp.sum((inv_ref[r] * y).T, axis=0, keepdims=True)


def block_sweep(inv, forcing, rows, first, count, coupling=None):
    blocks, width = forcing.shape[0], forcing.shape[2]
    at = lambda g, *_: (g + first, 0, 0)
    if coupling is None:
        operands = [inv, forcing]
        specs = [pl.BlockSpec((rows, width, width), at), pl.BlockSpec((rows, 1, width), at)]
        prefetch = 0
        bands = 0
    else:
        cols, tile, state, ghost, prows = coupling
        bands = tile.shape[1]
        operands = [cols, tile, inv, state, ghost, forcing, prows]
        specs = [
            pl.BlockSpec((rows, bands, width, width), lambda g, *_: (g + first, 0, 0, 0)),
            pl.BlockSpec((rows, width, width), at),
            pl.BlockSpec(state.shape, lambda g, *_: (0, 0, 0)),
            pl.BlockSpec(ghost.shape, lambda g, *_: (0, 0, 0)),
            pl.BlockSpec((rows, 1, width), at),
            pl.BlockSpec((rows, 1, width), at),
        ]
        prefetch = 1
    done = count * rows
    grid_spec = pltpu.PrefetchScalarGridSpec(
        num_scalar_prefetch=prefetch,
        grid=(count,),
        in_specs=specs,
        out_specs=pl.BlockSpec((rows, 1, width), lambda g, *_: (g, 0, 0)),
    )
    return pl.pallas_call(
        functools.partial(sweep_kernel, coupled_terms=coupling is not None, first=first, blocks=blocks),
        grid_spec=grid_spec,
        out_shape=jax.ShapeDtypeStruct((done, 1, width), jnp.float32),
        cost_estimate=pl.CostEstimate(
            flops=2 * done * width * width * (bands + 1),
            transcendentals=0,
            bytes_accessed=done * width * width * (2 * bands + 4),
        ),
    )(*operands)


def doubling_order(bits):
    if bits == 7:
        return [3, 5, 2, 6, 4, 1, 0]
    return list(range(bits - 1, -1, -1))


def exchange(outgoing, partners, tie=None, midway=None):
    count = lax.axis_size("sub")
    bits = count.bit_length() - 1
    me = lax.axis_index("sub")
    extra = None
    if tie is not None:
        outgoing, tie = lax.optimization_barrier((outgoing, tie))
    if 1 << bits != count:
        every = lax.all_gather(outgoing, "sub", axis=0, tiled=False)
        if midway is not None:
            extra = midway()
        return every[partners, jnp.arange(outgoing.shape[0])], extra
    order = doubling_order(bits)
    held = outgoing[None]
    for step, bit in enumerate(order):
        route = [(low, low ^ (1 << bit)) for low in range(count)]
        held = jnp.concatenate([held, lax.ppermute(held, "sub", route)], axis=0)
        if midway is not None and step == min(2, len(order) - 1):
            extra = midway()
            held, extra = lax.optimization_barrier((held, extra))
    flipped = partners ^ me
    entry = jnp.zeros_like(partners)
    for step, bit in enumerate(order):
        entry = entry | (((flipped >> bit) & 1) << step)
    return held[entry, jnp.arange(outgoing.shape[0])], extra


def per_device(
    recharge,
    inv_diag,
    couple,
    col_index,
    soil_id,
    field_id,
    robin_table,
    field_rate,
    matching,
    lambda_in,
):
    blocks = recharge.shape[2]
    width = recharge.shape[3]
    colours = lambda_in.shape[2]
    per_colour = lambda_in.shape[3]
    iface = colours * per_colour
    nitrate = (jnp.arange(width) >= width // 2).astype(jnp.float32)
    rate = jnp.take(field_rate, field_id[0, 0], axis=0)
    rhs = recharge[0, 0] + rate[:, None] * nitrate
    soil_hits = soil_id[0, 0][:, None] == jnp.arange(robin_table.shape[0], dtype=jnp.int32)[None, :]
    p_block = jnp.sum(jnp.where(soil_hits, robin_table[None, :], 0.0), axis=1)
    p_face = p_block[:iface]
    inverse = inv_diag[0, 0]
    columns = col_index[0, 0]
    partners = lax.dynamic_index_in_dim(matching, lax.axis_index("sub"), axis=1, keepdims=False)
    robin_data = lambda_in[0, 0]

    flat_columns = columns.reshape(-1)
    prows = jnp.concatenate([p_face, jnp.zeros((blocks - iface,), jnp.float32)])[:, None, None] * jnp.ones((1, 1, width), jnp.float32)

    def sweep_rows(state, ghost, forcing, rows, first, count):
        if state is None:
            return block_sweep(inverse, forcing, rows, first, count)
        coupling = (flat_columns, couple[0, 0], state, ghost, prows)
        return block_sweep(inverse, forcing, rows, first, count, coupling)

    head_forcing = rhs[:, None]
    head_source = lambda forcing: head_forcing if blocks - G >= iface else forcing
    pending = None
    body_rows = next(size for size in (20, 10, 8, 5, 4, 2, 1) if blocks % size == 0)
    state = None
    ghost = None
    for outer in range(OUTER):
        forcing = jnp.concatenate([rhs[:iface] + robin_data.reshape(iface, width), rhs[iface:]], axis=0)[:, None]
        for sweep in range(SWEEPS):
            if pending is not None:
                top, pending = pending, None
            else:
                top = sweep_rows(state, ghost, head_source(forcing), G, (blocks - G) // G, 1)
            sent = partner(top, "depth", 0)
            state = sweep_rows(state, ghost, forcing, body_rows, 0, blocks // body_rows)
            ghost = sent
        state2 = state[:, 0]
        outgoing = (
            2.0
            * p_face.reshape(colours, per_colour)[..., None]
            * state2[:iface].reshape(colours, per_colour, width)
            - robin_data
        )
        if outer < OUTER - 1 and blocks - G >= iface:
            ahead = lambda state=state, ghost=ghost: sweep_rows(state, ghost, head_forcing, G, (blocks - G) // G, 1)
            robin_data, pending = exchange(outgoing, partners, tie=top, midway=ahead)
        else:
            robin_data, _ = exchange(outgoing, partners)
    return (state[:, 0][None, None], robin_data[None, None])


def solution(mesh):
    placed = (
        P("sub", "depth", None, None),
        P("sub", "depth", None, None, None),
        P("sub", "depth", None, None, None, None),
        P("sub", "depth", None, None),
        P("sub", "depth", None),
        P("sub", "depth", None),
        P(),
        P(),
        P(),
        P("sub", "depth", None, None, None),
    )
    return jax.shard_map(
        per_device,
        mesh=mesh,
        in_specs=placed,
        out_specs=(P("sub", "depth", None, None), P("sub", "depth", None, None, None)),
        check_vma=False,
    )
```

```python
import functools

import jax
import jax.numpy as jnp
from jax import lax
from jax.experimental import pallas as pl
from jax.experimental.pallas import tpu as pltpu
from jax.sharding import PartitionSpec as P

G = 2
SWEEPS = 4
OUTER = 2


def partner(block, axis, bit):
    count = lax.axis_size(axis)
    route = []
    for low in range(count):
        high = low | 1 << bit
        if high != low and high < count:
            route += [(low, high), (high, low)]
    return lax.ppermute(block, axis, route)


def sweep_kernel(*refs, coupled_terms, first, blocks):
    if coupled_terms:
        cols_ref, c_ref, inv_ref, state_ref, ghost_ref, f_ref, p_ref, o_ref = refs
    else:
        inv_ref, f_ref, o_ref = refs
    rows = inv_ref.shape[0]
    base = (pl.program_id(0) + first) * rows
    for r in range(rows):
        y = f_ref[r]
        if coupled_terms:
            bands = c_ref.shape[1]
            row = base + r
            acc = None
            for b in range(bands):
                col = cols_ref[row * bands + b]
                own = state_ref[jnp.minimum(col, blocks - 1)]
                other = ghost_ref[jnp.maximum(col - blocks, 0)]
                xb = jnp.where(col >= blocks, other, own)
                term = c_ref[r, b].astype(jnp.float32) * xb
                acc = term if acc is None else acc + term
            y = y - jnp.sum(acc.T, axis=0, keepdims=True)
            y = y - p_ref[r] * state_ref[row]
        o_ref[r] = jnp.sum((inv_ref[r] * y).T, axis=0, keepdims=True)


def block_sweep(inv, forcing, rows, first, count, coupling=None):
    blocks, width = forcing.shape[0], forcing.shape[2]
    at = lambda g, *_: (g + first, 0, 0)
    if coupling is None:
        operands = [inv, forcing]
        specs = [pl.BlockSpec((rows, width, width), at), pl.BlockSpec((rows, 1, width), at)]
        prefetch = 0
        bands = 0
    else:
        cols, tile, state, ghost, prows = coupling
        bands = tile.shape[1]
        operands = [cols, tile, inv, state, ghost, forcing, prows]
        specs = [
            pl.BlockSpec((rows, bands, width, width), lambda g, *_: (g + first, 0, 0, 0)),
            pl.BlockSpec((rows, width, width), at),
            pl.BlockSpec(state.shape, lambda g, *_: (0, 0, 0)),
            pl.BlockSpec(ghost.shape, lambda g, *_: (0, 0, 0)),
            pl.BlockSpec((rows, 1, width), at),
            pl.BlockSpec((rows, 1, width), at),
        ]
        prefetch = 1
    done = count * rows
    grid_spec = pltpu.PrefetchScalarGridSpec(
        num_scalar_prefetch=prefetch,
        grid=(count,),
        in_specs=specs,
        out_specs=pl.BlockSpec((rows, 1, width), lambda g, *_: (g, 0, 0)),
    )
    return pl.pallas_call(
        functools.partial(sweep_kernel, coupled_terms=coupling is not None, first=first, blocks=blocks),
        grid_spec=grid_spec,
        out_shape=jax.ShapeDtypeStruct((done, 1, width), jnp.float32),
        cost_estimate=pl.CostEstimate(
            flops=2 * done * width * width * (bands + 1),
            transcendentals=0,
            bytes_accessed=done * width * width * (2 * bands + 4),
        ),
    )(*operands)


def head_kernel(cols_ref, c_ref, inv_ref, state_ref, ghost_ref, f_ref, o_ref, *, blocks):
    rows, bands = c_ref.shape[0], c_ref.shape[1]
    for r in range(rows):
        acc = None
        for b in range(bands):
            col = cols_ref[r * bands + b]
            own = state_ref[jnp.minimum(col, blocks - 1)]
            other = ghost_ref[jnp.maximum(col - blocks, 0)]
            xb = jnp.where(col >= blocks, other, own)
            term = c_ref[r, b].astype(jnp.float32) * xb
            acc = term if acc is None else acc + term
        y = f_ref[r] - jnp.sum(acc.T, axis=0, keepdims=True)
        o_ref[r] = jnp.sum((inv_ref[r] * y).T, axis=0, keepdims=True)


def head_sweep(cols, tile, inv, state, ghost, f):
    blocks, width = state.shape[0], state.shape[2]
    in_vmem = pl.BlockSpec(memory_space=pltpu.VMEM)
    in_smem = pl.BlockSpec(memory_space=pltpu.SMEM)
    return pl.pallas_call(
        functools.partial(head_kernel, blocks=blocks),
        in_specs=[in_smem, in_vmem, in_vmem, in_vmem, in_vmem, in_vmem],
        out_specs=in_vmem,
        out_shape=jax.ShapeDtypeStruct((tile.shape[0], 1, width), jnp.float32),
    )(cols, tile, inv, state, ghost, f)


def doubling_order(bits):
    if bits == 7:
        return [3, 5, 2, 6, 4, 1, 0]
    return list(range(bits - 1, -1, -1))


def exchange(outgoing, partners, tie=None, midway=None):
    count = lax.axis_size("sub")
    bits = count.bit_length() - 1
    me = lax.axis_index("sub")
    extra = None
    if tie is not None:
        outgoing, tie = lax.optimization_barrier((outgoing, tie))
    if 1 << bits != count:
        every = lax.all_gather(outgoing, "sub", axis=0, tiled=False)
        if midway is not None:
            extra = midway()
        return every[partners, jnp.arange(outgoing.shape[0])], extra
    order = doubling_order(bits)
    held = outgoing[None]
    for step, bit in enumerate(order):
        route = [(low, low ^ (1 << bit)) for low in range(count)]
        held = jnp.concatenate([held, lax.ppermute(held, "sub", route)], axis=0)
        if midway is not None and step == min(2, len(order) - 1):
            extra = midway()
            held, extra = lax.optimization_barrier((held, extra))
    flipped = partners ^ me
    entry = jnp.zeros_like(partners)
    for step, bit in enumerate(order):
        entry = entry | (((flipped >> bit) & 1) << step)
    return held[entry, jnp.arange(outgoing.shape[0])], extra


def per_device(
    recharge,
    inv_diag,
    couple,
    col_index,
    soil_id,
    field_id,
    robin_table,
    field_rate,
    matching,
    lambda_in,
):
    blocks = recharge.shape[2]
    width = recharge.shape[3]
    colours = lambda_in.shape[2]
    per_colour = lambda_in.shape[3]
    iface = colours * per_colour
    nitrate = (jnp.arange(width) >= width // 2).astype(jnp.float32)
    rate = jnp.take(field_rate, field_id[0, 0], axis=0)
    rhs = recharge[0, 0] + rate[:, None] * nitrate
    soil_hits = soil_id[0, 0][:, None] == jnp.arange(robin_table.shape[0], dtype=jnp.int32)[None, :]
    p_block = jnp.sum(jnp.where(soil_hits, robin_table[None, :], 0.0), axis=1)
    p_face = p_block[:iface]
    inverse = inv_diag[0, 0]
    columns = col_index[0, 0]
    partners = lax.dynamic_index_in_dim(matching, lax.axis_index("sub"), axis=1, keepdims=False)
    robin_data = lambda_in[0, 0]

    flat_columns = columns.reshape(-1)
    prows = jnp.concatenate([p_face, jnp.zeros((blocks - iface,), jnp.float32)])[:, None, None] * jnp.ones((1, 1, width), jnp.float32)

    bands = couple.shape[3]
    head_tables = (
        flat_columns[(blocks - G) * bands:],
        couple[0, 0, blocks - G:],
        inverse[blocks - G:],
    )

    def sweep_rows(state, ghost, forcing, rows, first, count):
        if state is not None and rows == G and first * G == blocks - G and blocks - G >= iface:
            return head_sweep(*head_tables, state, ghost, forcing[blocks - G:])
        if state is None:
            return block_sweep(inverse, forcing, rows, first, count)
        coupling = (flat_columns, couple[0, 0], state, ghost, prows)
        return block_sweep(inverse, forcing, rows, first, count, coupling)

    head_forcing = rhs[:, None]
    head_source = lambda forcing: head_forcing if blocks - G >= iface else forcing
    pending = None
    body_rows = next(size for size in (20, 10, 8, 5, 4, 2, 1) if blocks % size == 0)
    state = None
    ghost = None
    for outer in range(OUTER):
        forcing = jnp.concatenate([rhs[:iface] + robin_data.reshape(iface, width), rhs[iface:]], axis=0)[:, None]
        for sweep in range(SWEEPS):
            if pending is not None:
                top, pending = pending, None
            else:
                top = sweep_rows(state, ghost, head_source(forcing), G, (blocks - G) // G, 1)
            sent = partner(top, "depth", 0)
            state = sweep_rows(state, ghost, forcing, body_rows, 0, blocks // body_rows)
            ghost = sent
        state2 = state[:, 0]
        outgoing = (
            2.0
            * p_face.reshape(colours, per_colour)[..., None]
            * state2[:iface].reshape(colours, per_colour, width)
            - robin_data
        )
        if outer < OUTER - 1 and blocks - G >= iface:
            ahead = lambda state=state, ghost=ghost: sweep_rows(state, ghost, head_forcing, G, (blocks - G) // G, 1)
            robin_data, pending = exchange(outgoing, partners, tie=top, midway=ahead)
        else:
            robin_data, _ = exchange(outgoing, partners)
    return (state[:, 0][None, None], robin_data[None, None])


def solution(mesh):
    placed = (
        P("sub", "depth", None, None),
        P("sub", "depth", None, None, None),
        P("sub", "depth", None, None, None, None),
        P("sub", "depth", None, None),
        P("sub", "depth", None),
        P("sub", "depth", None),
        P(),
        P(),
        P(),
        P("sub", "depth", None, None, None),
    )
    return jax.shard_map(
        per_device,
        mesh=mesh,
        in_specs=placed,
        out_specs=(P("sub", "depth", None, None), P("sub", "depth", None, None, None)),
        check_vma=False,
    )
```

```python
import functools

import jax
import jax.numpy as jnp
from jax import lax
from jax.experimental import pallas as pl
from jax.experimental.pallas import tpu as pltpu
from jax.sharding import PartitionSpec as P

G = 2
SWEEPS = 4
OUTER = 2


def partner(block, axis, bit):
    count = lax.axis_size(axis)
    route = []
    for low in range(count):
        high = low | 1 << bit
        if high != low and high < count:
            route += [(low, high), (high, low)]
    return lax.ppermute(block, axis, route)


def sweep_kernel(*refs, coupled_terms, first, blocks):
    if coupled_terms:
        cols_ref, p_ref, c_ref, inv_ref, state_ref, ghost_ref, f_ref, o_ref = refs
    else:
        inv_ref, f_ref, o_ref = refs
    rows = inv_ref.shape[0]
    base = (pl.program_id(0) + first) * rows
    for r in range(rows):
        y = f_ref[r]
        if coupled_terms:
            bands = c_ref.shape[1]
            row = base + r
            acc = None
            for b in range(bands):
                col = cols_ref[row, b]
                own = state_ref[jnp.minimum(col, blocks - 1)]
                other = ghost_ref[jnp.maximum(col - blocks, 0)]
                xb = jnp.where(col >= blocks, other, own)
                term = c_ref[r, b].astype(jnp.float32) * xb
                acc = term if acc is None else acc + term
            y = y - jnp.sum(acc.T, axis=0, keepdims=True)
            y = y - p_ref[row] * state_ref[row]
        o_ref[r] = jnp.sum((inv_ref[r] * y).T, axis=0, keepdims=True)


def block_sweep(inv, forcing, rows, first, count, coupling=None):
    blocks, width = forcing.shape[0], forcing.shape[2]
    at = lambda g, *_: (g + first, 0, 0)
    if coupling is None:
        operands = [inv, forcing]
        specs = [pl.BlockSpec((rows, width, width), at), pl.BlockSpec((rows, 1, width), at)]
        prefetch = 0
        bands = 0
    else:
        cols, prows, tile, state, ghost = coupling
        bands = tile.shape[1]
        operands = [cols, prows, tile, inv, state, ghost, forcing]
        specs = [
            pl.BlockSpec((rows, bands, width, width), lambda g, *_: (g + first, 0, 0, 0)),
            pl.BlockSpec((rows, width, width), at),
            pl.BlockSpec(state.shape, lambda g, *_: (0, 0, 0)),
            pl.BlockSpec(ghost.shape, lambda g, *_: (0, 0, 0)),
            pl.BlockSpec((rows, 1, width), at),
        ]
        prefetch = 2
    done = count * rows
    grid_spec = pltpu.PrefetchScalarGridSpec(
        num_scalar_prefetch=prefetch,
        grid=(count,),
        in_specs=specs,
        out_specs=pl.BlockSpec((rows, 1, width), lambda g, *_: (g, 0, 0)),
    )
    return pl.pallas_call(
        functools.partial(sweep_kernel, coupled_terms=coupling is not None, first=first, blocks=blocks),
        grid_spec=grid_spec,
        out_shape=jax.ShapeDtypeStruct((done, 1, width), jnp.float32),
        cost_estimate=pl.CostEstimate(
            flops=2 * done * width * width * (bands + 1),
            transcendentals=0,
            bytes_accessed=done * width * width * (2 * bands + 4),
        ),
    )(*operands)


def doubling_order(bits):
    if bits == 7:
        return [3, 5, 2, 6, 4, 1, 0]
    return list(range(bits - 1, -1, -1))


def exchange(outgoing, partners, tie=None, midway=None):
    count = lax.axis_size("sub")
    bits = count.bit_length() - 1
    me = lax.axis_index("sub")
    extra = None
    if tie is not None:
        outgoing, tie = lax.optimization_barrier((outgoing, tie))
    if 1 << bits != count:
        every = lax.all_gather(outgoing, "sub", axis=0, tiled=False)
        if midway is not None:
            extra = midway()
        return every[partners, jnp.arange(outgoing.shape[0])], extra
    order = doubling_order(bits)
    held = outgoing[None]
    for step, bit in enumerate(order):
        route = [(low, low ^ (1 << bit)) for low in range(count)]
        held = jnp.concatenate([held, lax.ppermute(held, "sub", route)], axis=0)
        if midway is not None and step == min(2, len(order) - 1):
            extra = midway()
            held, extra = lax.optimization_barrier((held, extra))
    flipped = partners ^ me
    entry = jnp.zeros_like(partners)
    for step, bit in enumerate(order):
        entry = entry | (((flipped >> bit) & 1) << step)
    return held[entry, jnp.arange(outgoing.shape[0])], extra


def per_device(
    recharge,
    inv_diag,
    couple,
    col_index,
    soil_id,
    field_id,
    robin_table,
    field_rate,
    matching,
    lambda_in,
):
    blocks = recharge.shape[2]
    width = recharge.shape[3]
    colours = lambda_in.shape[2]
    per_colour = lambda_in.shape[3]
    iface = colours * per_colour
    nitrate = (jnp.arange(width) >= width // 2).astype(jnp.float32)
    rate = jnp.take(field_rate, field_id[0, 0], axis=0)
    rhs = recharge[0, 0] + rate[:, None] * nitrate
    soil_hits = soil_id[0, 0][:, None] == jnp.arange(robin_table.shape[0], dtype=jnp.int32)[None, :]
    p_block = jnp.sum(jnp.where(soil_hits, robin_table[None, :], 0.0), axis=1)
    p_face = p_block[:iface]
    inverse = inv_diag[0, 0]
    columns = col_index[0, 0]
    partners = lax.dynamic_index_in_dim(matching, lax.axis_index("sub"), axis=1, keepdims=False)
    robin_data = lambda_in[0, 0]

    prows = jnp.where(jnp.arange(blocks) < iface, p_block, 0.0)

    def sweep_rows(state, ghost, forcing, rows, first, count):
        if state is None:
            return block_sweep(inverse, forcing, rows, first, count)
        coupling = (columns, prows, couple[0, 0], state, ghost)
        return block_sweep(inverse, forcing, rows, first, count, coupling)

    head_forcing = rhs[:, None]
    head_source = lambda forcing: head_forcing if blocks - G >= iface else forcing
    pending = None
    body_rows = next(size for size in (20, 10, 8, 5, 4, 2, 1) if blocks % size == 0)
    state = None
    ghost = None
    for outer in range(OUTER):
        forcing = jnp.concatenate([rhs[:iface] + robin_data.reshape(iface, width), rhs[iface:]], axis=0)[:, None]
        for sweep in range(SWEEPS):
            if pending is not None:
                top, pending = pending, None
            else:
                top = sweep_rows(state, ghost, head_source(forcing), G, (blocks - G) // G, 1)
            sent = partner(top, "depth", 0)
            state = sweep_rows(state, ghost, forcing, body_rows, 0, blocks // body_rows)
            ghost = sent
        state2 = state[:, 0]
        outgoing = (
            2.0
            * p_face.reshape(colours, per_colour)[..., None]
            * state2[:iface].reshape(colours, per_colour, width)
            - robin_data
        )
        if outer < OUTER - 1 and blocks - G >= iface:
            ahead = lambda state=state, ghost=ghost: sweep_rows(state, ghost, head_forcing, G, (blocks - G) // G, 1)
            robin_data, pending = exchange(outgoing, partners, tie=top, midway=ahead)
        else:
            robin_data, _ = exchange(outgoing, partners)
    return (state[:, 0][None, None], robin_data[None, None])


def solution(mesh):
    placed = (
        P("sub", "depth", None, None),
        P("sub", "depth", None, None, None),
        P("sub", "depth", None, None, None, None),
        P("sub", "depth", None, None),
        P("sub", "depth", None),
        P("sub", "depth", None),
        P(),
        P(),
        P(),
        P("sub", "depth", None, None, None),
    )
    return jax.shard_map(
        per_device,
        mesh=mesh,
        in_specs=placed,
        out_specs=(P("sub", "depth", None, None), P("sub", "depth", None, None, None)),
        check_vma=False,
    )
```

```python
import functools

import jax
import jax.numpy as jnp
from jax import lax
from jax.experimental import pallas as pl
from jax.experimental.pallas import tpu as pltpu
from jax.sharding import PartitionSpec as P

G = 2
SWEEPS = 4
OUTER = 2


def partner(block, axis, bit):
    count = lax.axis_size(axis)
    route = []
    for low in range(count):
        high = low | 1 << bit
        if high != low and high < count:
            route += [(low, high), (high, low)]
    return lax.ppermute(block, axis, route)


def sweep_kernel(*refs, coupled_terms, first, blocks):
    if coupled_terms:
        cols_ref, c_ref, inv_ref, state_ref, ghost_ref, f_ref, p_ref, o_ref = refs
    else:
        inv_ref, f_ref, o_ref = refs
    rows = inv_ref.shape[0]
    base = (pl.program_id(0) + first) * rows
    for r in range(rows):
        y = f_ref[r]
        if coupled_terms:
            bands = c_ref.shape[1]
            row = base + r
            acc = None
            for b in range(bands):
                col = cols_ref[row * bands + b]
                own = state_ref[jnp.minimum(col, blocks - 1)]
                other = ghost_ref[jnp.maximum(col - blocks, 0)]
                xb = jnp.where(col >= blocks, other, own)
                term = c_ref[r, b].astype(jnp.float32) * xb
                acc = term if acc is None else acc + term
            y = y - jnp.sum(acc.T, axis=0, keepdims=True)
            y = y - p_ref[r] * state_ref[row]
        o_ref[r] = jnp.sum((inv_ref[r] * y).T, axis=0, keepdims=True)


def block_sweep(inv, forcing, rows, first, count, coupling=None):
    blocks, width = forcing.shape[0], forcing.shape[2]
    at = lambda g, *_: (g + first, 0, 0)
    if coupling is None:
        operands = [inv, forcing]
        specs = [pl.BlockSpec((rows, width, width), at), pl.BlockSpec((rows, 1, width), at)]
        prefetch = 0
        bands = 0
    else:
        cols, tile, state, ghost, prows = coupling
        bands = tile.shape[1]
        operands = [cols, tile, inv, state, ghost, forcing, prows]
        specs = [
            pl.BlockSpec((rows, bands, width, width), lambda g, *_: (g + first, 0, 0, 0)),
            pl.BlockSpec((rows, width, width), at),
            pl.BlockSpec(state.shape, lambda g, *_: (0, 0, 0)),
            pl.BlockSpec(ghost.shape, lambda g, *_: (0, 0, 0)),
            pl.BlockSpec((rows, 1, width), at),
            pl.BlockSpec((rows, 1, width), at),
        ]
        prefetch = 1
    done = count * rows
    grid_spec = pltpu.PrefetchScalarGridSpec(
        num_scalar_prefetch=prefetch,
        grid=(count,),
        in_specs=specs,
        out_specs=pl.BlockSpec((rows, 1, width), lambda g, *_: (g, 0, 0)),
    )
    return pl.pallas_call(
        functools.partial(sweep_kernel, coupled_terms=coupling is not None, first=first, blocks=blocks),
        grid_spec=grid_spec,
        out_shape=jax.ShapeDtypeStruct((done, 1, width), jnp.float32),
        cost_estimate=pl.CostEstimate(
            flops=2 * done * width * width * (bands + 1),
            transcendentals=0,
            bytes_accessed=done * width * width * (2 * bands + 4),
        ),
    )(*operands)


def doubling_order(bits):
    if bits == 7:
        return [3, 5, 2, 6, 4, 1, 0]
    return list(range(bits - 1, -1, -1))


def exchange(outgoing, partners, matching_rows, tie=None, midway=None):
    count = lax.axis_size("sub")
    bits = count.bit_length() - 1
    me = lax.axis_index("sub")
    extra = None
    if tie is not None:
        outgoing, tie = lax.optimization_barrier((outgoing, tie))
    if 1 << bits != count:
        every = lax.all_gather(outgoing, "sub", axis=0, tiled=False)
        if midway is not None:
            extra = midway()
        return every[partners, jnp.arange(outgoing.shape[0])], extra
    order = doubling_order(bits)
    held = outgoing[None]
    for step, bit in enumerate(order[:-1]):
        route = [(low, low ^ (1 << bit)) for low in range(count)]
        held = jnp.concatenate([held, lax.ppermute(held, "sub", route)], axis=0)
        if midway is not None and step == min(2, len(order) - 1):
            extra = midway()
            held, extra = lax.optimization_barrier((held, extra))
    last = order[-1]
    colours = jnp.arange(outgoing.shape[0])

    def located(targets):
        flipped = targets ^ me
        entry = jnp.zeros_like(targets)
        for step, bit in enumerate(order[:-1]):
            entry = entry | (((flipped >> bit) & 1) << step)
        return held[entry, colours], ((flipped >> last) & 1) == 0

    wanted = lax.dynamic_index_in_dim(matching_rows, me ^ (1 << last), axis=1, keepdims=False)
    offer, have = located(wanted)
    route = [(low, low ^ (1 << last)) for low in range(count)]
    passed = lax.ppermute(jnp.where(have[:, None, None], offer, 0.0), "sub", route)
    own, mine = located(partners)
    return jnp.where(mine[:, None, None], own, passed), extra


def per_device(
    recharge,
    inv_diag,
    couple,
    col_index,
    soil_id,
    field_id,
    robin_table,
    field_rate,
    matching,
    lambda_in,
):
    blocks = recharge.shape[2]
    width = recharge.shape[3]
    colours = lambda_in.shape[2]
    per_colour = lambda_in.shape[3]
    iface = colours * per_colour
    nitrate = (jnp.arange(width) >= width // 2).astype(jnp.float32)
    rate = jnp.take(field_rate, field_id[0, 0], axis=0)
    rhs = recharge[0, 0] + rate[:, None] * nitrate
    soil_hits = soil_id[0, 0][:, None] == jnp.arange(robin_table.shape[0], dtype=jnp.int32)[None, :]
    p_block = jnp.sum(jnp.where(soil_hits, robin_table[None, :], 0.0), axis=1)
    p_face = p_block[:iface]
    inverse = inv_diag[0, 0]
    columns = col_index[0, 0]
    partners = lax.dynamic_index_in_dim(matching, lax.axis_index("sub"), axis=1, keepdims=False)
    robin_data = lambda_in[0, 0]

    flat_columns = columns.reshape(-1)
    prows = jnp.concatenate([p_face, jnp.zeros((blocks - iface,), jnp.float32)])[:, None, None] * jnp.ones((1, 1, width), jnp.float32)

    def sweep_rows(state, ghost, forcing, rows, first, count):
        if state is None:
            return block_sweep(inverse, forcing, rows, first, count)
        coupling = (flat_columns, couple[0, 0], state, ghost, prows)
        return block_sweep(inverse, forcing, rows, first, count, coupling)

    head_forcing = rhs[:, None]
    head_source = lambda forcing: head_forcing if blocks - G >= iface else forcing
    pending = None
    body_rows = next(size for size in (20, 10, 8, 5, 4, 2, 1) if blocks % size == 0)
    state = None
    ghost = None
    for outer in range(OUTER):
        forcing = jnp.concatenate([rhs[:iface] + robin_data.reshape(iface, width), rhs[iface:]], axis=0)[:, None]
        for sweep in range(SWEEPS):
            if pending is not None:
                top, pending = pending, None
            else:
                top = sweep_rows(state, ghost, head_source(forcing), G, (blocks - G) // G, 1)
            sent = partner(top, "depth", 0)
            state = sweep_rows(state, ghost, forcing, body_rows, 0, blocks // body_rows)
            ghost = sent
        state2 = state[:, 0]
        outgoing = (
            2.0
            * p_face.reshape(colours, per_colour)[..., None]
            * state2[:iface].reshape(colours, per_colour, width)
            - robin_data
        )
        if outer < OUTER - 1 and blocks - G >= iface:
            ahead = lambda state=state, ghost=ghost: sweep_rows(state, ghost, head_forcing, G, (blocks - G) // G, 1)
            robin_data, pending = exchange(outgoing, partners, matching, tie=top, midway=ahead)
        else:
            robin_data, _ = exchange(outgoing, partners, matching)
    return (state[:, 0][None, None], robin_data[None, None])


def solution(mesh):
    placed = (
        P("sub", "depth", None, None),
        P("sub", "depth", None, None, None),
        P("sub", "depth", None, None, None, None),
        P("sub", "depth", None, None),
        P("sub", "depth", None),
        P("sub", "depth", None),
        P(),
        P(),
        P(),
        P("sub", "depth", None, None, None),
    )
    return jax.shard_map(
        per_device,
        mesh=mesh,
        in_specs=placed,
        out_specs=(P("sub", "depth", None, None), P("sub", "depth", None, None, None)),
        check_vma=False,
    )
```

```python
import functools

import jax
import jax.numpy as jnp
from jax import lax
from jax.experimental import pallas as pl
from jax.experimental.pallas import tpu as pltpu
from jax.sharding import PartitionSpec as P

G = 2
SWEEPS = 4
OUTER = 2


def partner(block, axis, bit):
    count = lax.axis_size(axis)
    route = []
    for low in range(count):
        high = low | 1 << bit
        if high != low and high < count:
            route += [(low, high), (high, low)]
    return lax.ppermute(block, axis, route)


def sweep_kernel(*refs, coupled_terms, first, blocks):
    if coupled_terms:
        cols_ref, c_ref, inv_ref, state_ref, ghost_ref, f_ref, p_ref, o_ref = refs
    else:
        inv_ref, f_ref, o_ref = refs
    rows = inv_ref.shape[0]
    base = (pl.program_id(0) + first) * rows
    for r in range(rows):
        y = f_ref[r]
        if coupled_terms:
            bands = c_ref.shape[1]
            row = base + r
            acc = None
            for b in range(bands):
                col = cols_ref[row * bands + b]
                own = state_ref[jnp.minimum(col, blocks - 1)]
                other = ghost_ref[jnp.maximum(col - blocks, 0)]
                xb = jnp.where(col >= blocks, other, own)
                term = c_ref[r, b].astype(jnp.float32) * xb
                acc = term if acc is None else acc + term
            y = y - jnp.sum(acc.T, axis=0, keepdims=True)
            y = y - p_ref[r] * state_ref[row]
        o_ref[r] = jnp.sum((inv_ref[r] * y).T, axis=0, keepdims=True)


def block_sweep(inv, forcing, rows, first, count, coupling=None):
    blocks, width = forcing.shape[0], forcing.shape[2]
    at = lambda g, *_: (g + first, 0, 0)
    if coupling is None:
        operands = [inv, forcing]
        specs = [pl.BlockSpec((rows, width, width), at), pl.BlockSpec((rows, 1, width), at)]
        prefetch = 0
        bands = 0
    else:
        cols, tile, state, ghost, prows = coupling
        bands = tile.shape[1]
        operands = [cols, tile, inv, state, ghost, forcing, prows]
        specs = [
            pl.BlockSpec((rows, bands, width, width), lambda g, *_: (g + first, 0, 0, 0)),
            pl.BlockSpec((rows, width, width), at),
            pl.BlockSpec(state.shape, lambda g, *_: (0, 0, 0)),
            pl.BlockSpec(ghost.shape, lambda g, *_: (0, 0, 0)),
            pl.BlockSpec((rows, 1, width), at),
            pl.BlockSpec((rows, 1, width), at),
        ]
        prefetch = 1
    done = count * rows
    grid_spec = pltpu.PrefetchScalarGridSpec(
        num_scalar_prefetch=prefetch,
        grid=(count,),
        in_specs=specs,
        out_specs=pl.BlockSpec((rows, 1, width), lambda g, *_: (g, 0, 0)),
    )
    return pl.pallas_call(
        functools.partial(sweep_kernel, coupled_terms=coupling is not None, first=first, blocks=blocks),
        grid_spec=grid_spec,
        out_shape=jax.ShapeDtypeStruct((done, 1, width), jnp.float32),
        cost_estimate=pl.CostEstimate(
            flops=2 * done * width * width * (bands + 1),
            transcendentals=0,
            bytes_accessed=done * width * width * (2 * bands + 4),
        ),
    )(*operands)


def doubling_order(bits):
    if bits == 7:
        return [0, 1, 4, 6, 2, 5, 3]
    return list(range(bits - 1, -1, -1))


def exchange(outgoing, partners, tie=None, midway=None):
    count = lax.axis_size("sub")
    bits = count.bit_length() - 1
    me = lax.axis_index("sub")
    extra = None
    if tie is not None:
        outgoing, tie = lax.optimization_barrier((outgoing, tie))
    if 1 << bits != count:
        every = lax.all_gather(outgoing, "sub", axis=0, tiled=False)
        if midway is not None:
            extra = midway()
        return every[partners, jnp.arange(outgoing.shape[0])], extra
    order = doubling_order(bits)
    held = outgoing[None]
    for step, bit in enumerate(order):
        route = [(low, low ^ (1 << bit)) for low in range(count)]
        held = jnp.concatenate([held, lax.ppermute(held, "sub", route)], axis=0)
        if midway is not None and step == min(2, len(order) - 1):
            extra = midway()
            held, extra = lax.optimization_barrier((held, extra))
    flipped = partners ^ me
    entry = jnp.zeros_like(partners)
    for step, bit in enumerate(order):
        entry = entry | (((flipped >> bit) & 1) << step)
    return held[entry, jnp.arange(outgoing.shape[0])], extra


def per_device(
    recharge,
    inv_diag,
    couple,
    col_index,
    soil_id,
    field_id,
    robin_table,
    field_rate,
    matching,
    lambda_in,
):
    blocks = recharge.shape[2]
    width = recharge.shape[3]
    colours = lambda_in.shape[2]
    per_colour = lambda_in.shape[3]
    iface = colours * per_colour
    nitrate = (jnp.arange(width) >= width // 2).astype(jnp.float32)
    rate = jnp.take(field_rate, field_id[0, 0], axis=0)
    rhs = recharge[0, 0] + rate[:, None] * nitrate
    soil_hits = soil_id[0, 0][:, None] == jnp.arange(robin_table.shape[0], dtype=jnp.int32)[None, :]
    p_block = jnp.sum(jnp.where(soil_hits, robin_table[None, :], 0.0), axis=1)
    p_face = p_block[:iface]
    inverse = inv_diag[0, 0]
    columns = col_index[0, 0]
    partners = lax.dynamic_index_in_dim(matching, lax.axis_index("sub"), axis=1, keepdims=False)
    robin_data = lambda_in[0, 0]

    flat_columns = columns.reshape(-1)
    prows = jnp.concatenate([p_face, jnp.zeros((blocks - iface,), jnp.float32)])[:, None, None] * jnp.ones((1, 1, width), jnp.float32)

    def sweep_rows(state, ghost, forcing, rows, first, count):
        if state is None:
            return block_sweep(inverse, forcing, rows, first, count)
        coupling = (flat_columns, couple[0, 0], state, ghost, prows)
        return block_sweep(inverse, forcing, rows, first, count, coupling)

    head_forcing = rhs[:, None]
    head_source = lambda forcing: head_forcing if blocks - G >= iface else forcing
    pending = None
    body_rows = next(size for size in (20, 10, 8, 5, 4, 2, 1) if blocks % size == 0)
    state = None
    ghost = None
    for outer in range(OUTER):
        forcing = jnp.concatenate([rhs[:iface] + robin_data.reshape(iface, width), rhs[iface:]], axis=0)[:, None]
        for sweep in range(SWEEPS):
            if pending is not None:
                top, pending = pending, None
            else:
                top = sweep_rows(state, ghost, head_source(forcing), G, (blocks - G) // G, 1)
            sent = partner(top, "depth", 0)
            state = sweep_rows(state, ghost, forcing, body_rows, 0, blocks // body_rows)
            ghost = sent
        state2 = state[:, 0]
        outgoing = (
            2.0
            * p_face.reshape(colours, per_colour)[..., None]
            * state2[:iface].reshape(colours, per_colour, width)
            - robin_data
        )
        if outer < OUTER - 1 and blocks - G >= iface:
            ahead = lambda state=state, ghost=ghost: sweep_rows(state, ghost, head_forcing, G, (blocks - G) // G, 1)
            robin_data, pending = exchange(outgoing, partners, tie=top, midway=ahead)
        else:
            robin_data, _ = exchange(outgoing, partners)
    return (state[:, 0][None, None], robin_data[None, None])


def solution(mesh):
    placed = (
        P("sub", "depth", None, None),
        P("sub", "depth", None, None, None),
        P("sub", "depth", None, None, None, None),
        P("sub", "depth", None, None),
        P("sub", "depth", None),
        P("sub", "depth", None),
        P(),
        P(),
        P(),
        P("sub", "depth", None, None, None),
    )
    return jax.shard_map(
        per_device,
        mesh=mesh,
        in_specs=placed,
        out_specs=(P("sub", "depth", None, None), P("sub", "depth", None, None, None)),
        check_vma=False,
    )
```

```python
import functools

import jax
import jax.numpy as jnp
from jax import lax
from jax.experimental import pallas as pl
from jax.experimental.pallas import tpu as pltpu
from jax.sharding import PartitionSpec as P

G = 2
SWEEPS = 4
OUTER = 2


def partner(block, axis, bit):
    count = lax.axis_size(axis)
    route = []
    for low in range(count):
        high = low | 1 << bit
        if high != low and high < count:
            route += [(low, high), (high, low)]
    return lax.ppermute(block, axis, route)


def sweep_kernel(*refs, coupled_terms, first, blocks):
    if coupled_terms:
        cols_ref, c_ref, inv_ref, state_ref, ghost_ref, f_ref, p_ref, o_ref = refs
    else:
        inv_ref, f_ref, o_ref = refs
    rows = inv_ref.shape[0]
    base = (pl.program_id(0) + first) * rows
    for r in range(rows):
        y = f_ref[r]
        if coupled_terms:
            bands = c_ref.shape[1]
            row = base + r
            acc = None
            for b in range(bands):
                col = cols_ref[row * bands + b]
                own = state_ref[jnp.minimum(col, blocks - 1)]
                other = ghost_ref[jnp.maximum(col - blocks, 0)]
                xb = jnp.where(col >= blocks, other, own)
                term = c_ref[r, b].astype(jnp.float32) * xb
                acc = term if acc is None else acc + term
            y = y - jnp.sum(acc.T, axis=0, keepdims=True)
            y = y - p_ref[r] * state_ref[row]
        o_ref[r] = jnp.sum((inv_ref[r] * y).T, axis=0, keepdims=True)


def block_sweep(inv, forcing, rows, first, count, coupling=None):
    blocks, width = forcing.shape[0], forcing.shape[2]
    at = lambda g, *_: (g + first, 0, 0)
    if coupling is None:
        operands = [inv, forcing]
        specs = [pl.BlockSpec((rows, width, width), at), pl.BlockSpec((rows, 1, width), at)]
        prefetch = 0
        bands = 0
    else:
        cols, tile, state, ghost, prows = coupling
        bands = tile.shape[1]
        operands = [cols, tile, inv, state, ghost, forcing, prows]
        specs = [
            pl.BlockSpec((rows, bands, width, width), lambda g, *_: (g + first, 0, 0, 0)),
            pl.BlockSpec((rows, width, width), at),
            pl.BlockSpec(state.shape, lambda g, *_: (0, 0, 0)),
            pl.BlockSpec(ghost.shape, lambda g, *_: (0, 0, 0)),
            pl.BlockSpec((rows, 1, width), at),
            pl.BlockSpec((rows, 1, width), at),
        ]
        prefetch = 1
    done = count * rows
    grid_spec = pltpu.PrefetchScalarGridSpec(
        num_scalar_prefetch=prefetch,
        grid=(count,),
        in_specs=specs,
        out_specs=pl.BlockSpec((rows, 1, width), lambda g, *_: (g, 0, 0)),
    )
    return pl.pallas_call(
        functools.partial(sweep_kernel, coupled_terms=coupling is not None, first=first, blocks=blocks),
        grid_spec=grid_spec,
        out_shape=jax.ShapeDtypeStruct((done, 1, width), jnp.float32),
        cost_estimate=pl.CostEstimate(
            flops=2 * done * width * width * (bands + 1),
            transcendentals=0,
            bytes_accessed=done * width * width * (2 * bands + 4),
        ),
    )(*operands)


def doubling_order(bits):
    if bits == 7:
        return [3, 5, 2, 6, 4, 1, 0]
    return list(range(bits - 1, -1, -1))


def exchange(outgoing, partners, tie=None, midway=None):
    count = lax.axis_size("sub")
    bits = count.bit_length() - 1
    me = lax.axis_index("sub")
    extra = None
    if tie is not None:
        outgoing, tie = lax.optimization_barrier((outgoing, tie))
    if 1 << bits != count:
        every = lax.all_gather(outgoing, "sub", axis=0, tiled=False)
        if midway is not None:
            extra = midway()
        return every[partners, jnp.arange(outgoing.shape[0])], extra
    order = doubling_order(bits)
    held = outgoing[None]
    for step, bit in enumerate(order):
        route = [(low, low ^ (1 << bit)) for low in range(count)]
        held = jnp.concatenate([held, lax.ppermute(held, "sub", route)], axis=0)
        if midway is not None and step == min(2, len(order) - 1):
            extra = midway()
            held, extra = lax.optimization_barrier((held, extra))
    flipped = partners ^ me
    entry = jnp.zeros_like(partners)
    for step, bit in enumerate(order):
        entry = entry | (((flipped >> bit) & 1) << step)
    return held[entry, jnp.arange(outgoing.shape[0])], extra


def per_device(
    recharge,
    inv_diag,
    couple,
    col_index,
    soil_id,
    field_id,
    robin_table,
    field_rate,
    matching,
    lambda_in,
):
    blocks = recharge.shape[2]
    width = recharge.shape[3]
    colours = lambda_in.shape[2]
    per_colour = lambda_in.shape[3]
    iface = colours * per_colour
    nitrate = (jnp.arange(width) >= width // 2).astype(jnp.float32)
    rate = jnp.take(field_rate, field_id[0, 0], axis=0)
    rhs = recharge[0, 0] + rate[:, None] * nitrate
    soil_hits = soil_id[0, 0][:, None] == jnp.arange(robin_table.shape[0], dtype=jnp.int32)[None, :]
    p_block = jnp.sum(jnp.where(soil_hits, robin_table[None, :], 0.0), axis=1)
    p_face = p_block[:iface]
    inverse = inv_diag[0, 0]
    columns = col_index[0, 0]
    partners = lax.dynamic_index_in_dim(matching, lax.axis_index("sub"), axis=1, keepdims=False)
    robin_data = lambda_in[0, 0]

    flat_columns = columns.reshape(-1)
    prows = jnp.concatenate([p_face, jnp.zeros((blocks - iface,), jnp.float32)])[:, None, None] * jnp.ones((1, 1, width), jnp.float32)

    def sweep_rows(state, ghost, forcing, rows, first, count):
        if state is None:
            return block_sweep(inverse, forcing, rows, first, count)
        coupling = (flat_columns, couple[0, 0], state, ghost, prows)
        return block_sweep(inverse, forcing, rows, first, count, coupling)

    head_forcing = rhs[:, None]
    head_source = lambda forcing: head_forcing if blocks - G >= iface else forcing
    pending = None
    body_rows = next(size for size in (20, 10, 8, 5, 4, 2, 1) if blocks % size == 0)
    state = None
    ghost = None
    for outer in range(OUTER):
        forcing = jnp.concatenate([rhs[:iface] + robin_data.reshape(iface, width), rhs[iface:]], axis=0)[:, None]
        for sweep in range(SWEEPS):
            if pending is not None:
                top, pending = pending, None
            else:
                top = sweep_rows(state, ghost, head_source(forcing), G, (blocks - G) // G, 1)
            sent = partner(top, "depth", 0)
            size = blocks if state is None else body_rows
            state = sweep_rows(state, ghost, forcing, size, 0, blocks // size)
            ghost = sent
        state2 = state[:, 0]
        outgoing = (
            2.0
            * p_face.reshape(colours, per_colour)[..., None]
            * state2[:iface].reshape(colours, per_colour, width)
            - robin_data
        )
        if outer < OUTER - 1 and blocks - G >= iface:
            ahead = lambda state=state, ghost=ghost: sweep_rows(state, ghost, head_forcing, G, (blocks - G) // G, 1)
            robin_data, pending = exchange(outgoing, partners, tie=top, midway=ahead)
        else:
            robin_data, _ = exchange(outgoing, partners)
    return (state[:, 0][None, None], robin_data[None, None])


def solution(mesh):
    placed = (
        P("sub", "depth", None, None),
        P("sub", "depth", None, None, None),
        P("sub", "depth", None, None, None, None),
        P("sub", "depth", None, None),
        P("sub", "depth", None),
        P("sub", "depth", None),
        P(),
        P(),
        P(),
        P("sub", "depth", None, None, None),
    )
    return jax.shard_map(
        per_device,
        mesh=mesh,
        in_specs=placed,
        out_specs=(P("sub", "depth", None, None), P("sub", "depth", None, None, None)),
        check_vma=False,
    )
```
